32 devices in a mesh: blk: 8 (over z, y), uly: 4 (over x, core).
Axes of the slice: x: 2, y: 2, z: 4, core: 2. Of those that a mesh axis runs over, the one named last changes fastest.
Arguments:
- tokens: bfloat16 [8, 16, 8, 1024], P('blk', None, 'uly'), may hold values from -12 to 12, as said below
- conv_weight: float32 [27, 1024], replicated, may hold values from -1.2 to 1.2
- conv_bias: float32 [1024], replicated, may hold values from -3 to 3
- qkv_weight: bfloat16 [3072, 1024], P('uly'), may hold values from -0.25 to 0.25
- out_weight: bfloat16 [1024, 1024], P('uly'), may hold values from -1.5 to 1.5
Outputs:
- attended_out: bfloat16 [8, 16, 8, 1024], P('blk', None, 'uly')
The draws below stay inside these ranges and needn't reach their ends.
Inputs may be any that keep to these rules, and one draw needn't show every extreme that they name: `tokens`: patch embeddings of the subvolume.
All inputs are finite; a program needn't handle non-finite values.
Results may differ from the reference program's by a relative error of at most 0.012.
The reference program's roundings to bfloat16 on the way (of `positioned`, `projected`, `weights` and `attended`) count: a program that leaves them out, or rounds other values in their place, can miss the bound.
Values may be sent and summed in bfloat16 or wider, within the bound.
No kernel may reach another device: no remote copies, remote signals or barrier semaphores. Data moves between devices by JAX's collectives and lax.ppermute only.
A program may use at most 64 MiB of HBM per device.

```python
import math
import jax
import jax.numpy as jnp
from jax import lax

D = 1024
H = 16
HS = 64
NX = 16
NY = 8
NZ = 8
TOKENS = 1024


def draw_tokens(key, part):
    array_shape = (NZ, NX, NY, D)
    first_key = jax.random.fold_in(key, 11)
    return jnp.clip(jax.random.normal(first_key, array_shape, jnp.float32), -6.0, 6.0).astype(jnp.bfloat16)


def levels(rng, shape, pieces, least, top_value):
    level = 1.0
    for dim, blocks in pieces:
        heights = jax.random.uniform(jax.random.fold_in(jax.random.fold_in(rng, 6), dim), (blocks,), jnp.float32, least / len(pieces), top_value / len(pieces))
        level = level * jnp.repeat(jnp.exp(heights), shape[dim] // blocks).reshape((-1,) + (1,) * (len(shape) - 1 - dim))
    return level


def gaussian(own_key, extent, width, reach, split=(), kind=jnp.bfloat16):
    entries = width * jax.random.normal(own_key, extent, jnp.float32)
    if split:
        entries = entries * levels(own_key, extent, split, -0.22, 0.18)
    return jnp.clip(entries, -reach, reach).astype(kind)


def setup_inputs(seed: int = 0) -> dict:
    streams_of = jax.random.split(jax.random.key(seed), 6)
    return {
        "tokens": draw_tokens(jax.random.fold_in(streams_of[5], 71), 0),
        "conv_weight": gaussian(streams_of[1], (27, D), 0.2, 1.2, (), jnp.float32),
        "conv_bias": gaussian(streams_of[2], (D,), 0.5, 3.0, (), jnp.float32),
        "qkv_weight": gaussian(streams_of[3], (3 * H * HS, D), (D // 2) ** -0.5, 0.25, ((0, 4),)),
        "out_weight": gaussian(streams_of[4], (H * HS, D), (H * HS // 64) ** -0.5, 1.5, ((0, 4),)),
    }


def convolve(tokens, conv_weight, conv_bias):
    values32 = tokens.astype(jnp.float32)
    padded = jnp.pad(values32, ((1, 1), (1, 1), (1, 1), (0, 0)))
    summed = values32 + conv_bias
    for step_z in range(3):
        for step_x in range(3):
            for step_y in range(3):
                summed = summed + conv_weight[9 * step_z + 3 * step_x + step_y] * padded[step_z:step_z + NZ, step_x:step_x + NX, step_y:step_y + NY]
    return summed.astype(jnp.bfloat16)

def attend_head(head_data):
    queries = head_data[0]
    key_rows = head_data[1]
    val_rows = head_data[2]
    score_scale = 1.0 / math.sqrt(HS)
    block_rows = math.gcd(TOKENS, 512)

    def query_block(query_part):
        scores = jnp.dot(query_part, key_rows.T, preferred_element_type=jnp.float32) * score_scale
        row_max = lax.optimization_barrier(jnp.max(scores, axis=1, keepdims=True))
        weights = jnp.exp(scores - row_max)
        row_sum = lax.optimization_barrier(jnp.sum(weights, axis=1, keepdims=True))
        mixed_rows = jnp.dot(weights.astype(jnp.bfloat16), val_rows, preferred_element_type=jnp.float32)
        return (mixed_rows / row_sum).astype(jnp.bfloat16)
    blocks = lax.map(query_block, queries.reshape(TOKENS // block_rows, block_rows, HS))
    return blocks.reshape(TOKENS, HS)

def reference(tokens, conv_weight, conv_bias, qkv_weight, out_weight):
    positioned = convolve(tokens, conv_weight, conv_bias).reshape(TOKENS, D)
    projected = jnp.dot(positioned, qkv_weight.T, preferred_element_type=jnp.float32).astype(jnp.bfloat16)
    per_head = projected.reshape(TOKENS, H, 3, HS).transpose(1, 2, 0, 3)
    attended = lax.map(attend_head, per_head)
    joined = attended.transpose(1, 0, 2).reshape(TOKENS, H * HS)
    output = jnp.dot(joined, out_weight, preferred_element_type=jnp.float32).astype(jnp.bfloat16)
    return output.reshape(NZ, NX, NY, D)
```

```python
import math

import jax
import jax.numpy as jnp
from jax import lax
from jax.sharding import PartitionSpec as P

HS = 64


def padded_2(shard, sides, width):
    for axis, dim in sides:
        size, length = (lax.axis_size(axis), shard.shape[dim])
        up = [(i, (i + 1) % size) for i in range(size - 1)]
        down = [(j, i) for i, j in up]
        last = lax.slice_in_dim(shard, length - width, length, axis=dim)
        initial = lax.slice_in_dim(shard, 0, width, axis=dim)
        before = lax.ppermute(last, axis, up)
        after = lax.ppermute(initial, axis, down)
        shard = jnp.concatenate([before, shard, after], axis=dim)
    return shard


def times_transposed(left, right):
    return lax.dot_general(
        left, right, (((1,), (1,)), ((), ())), preferred_element_type=jnp.float32
    )


def on_device(tokens, conv_weight, conv_bias, qkv_weight, out_weight):
    z_count, x_count, y_count, features = tokens.shape
    padded = padded_2(tokens, (("blk", 0), ("uly", 2)), 1)
    padded = jnp.pad(padded, ((0, 0), (1, 1), (0, 0), (0, 0)))
    summed = tokens.astype(jnp.float32) + conv_bias
    for step_z in range(3):
        for step_x in range(3):
            for step_y in range(3):
                summed = (
                    summed
                    + conv_weight[9 * step_z + 3 * step_x + step_y]
                    * padded[
                        step_z : step_z + z_count,
                        step_x : step_x + x_count,
                        step_y : step_y + y_count,
                    ]
                )
    token_rows = summed.astype(jnp.bfloat16).reshape(-1, features)
    local_tok = token_rows.shape[0]
    heads_here = qkv_weight.shape[0] // (3 * HS)
    slab_rows = lax.all_gather(token_rows, "uly", axis=0, tiled=True)
    slab_tok = slab_rows.shape[0]
    projected = times_transposed(slab_rows, qkv_weight).astype(jnp.bfloat16)
    split_heads = projected.reshape(slab_tok, heads_here, 3, HS)
    queries = split_heads[:, :, 0]
    key_rows = split_heads[:, :, 1]
    val_rows = split_heads[:, :, 2]
    score_scale = 1.0 / math.sqrt(HS)

    def key_block(carry_state, key_value):
        running_max, running_sum, weighted = carry_state
        key_part, value_part = key_value
        scores = (
            jnp.einsum("qhd,khd->hqk", queries, key_part, preferred_element_type=jnp.float32)
            * score_scale
        )
        new_max = jnp.maximum(running_max, jnp.max(scores, axis=2))
        shrink = jnp.exp(running_max - new_max)
        weights = jnp.exp(scores - new_max[:, :, None])
        running_sum = running_sum * shrink + jnp.sum(weights, axis=2)
        weighted = weighted * shrink[:, :, None] + jnp.einsum(
            "hqk,khd->hqd",
            weights.astype(jnp.bfloat16),
            value_part,
            preferred_element_type=jnp.float32,
        )
        return ((new_max, running_sum, weighted), None)

    start_state = (
        jnp.full((heads_here, slab_tok), -1e30, jnp.float32),
        jnp.zeros((heads_here, slab_tok), jnp.float32),
        jnp.zeros((heads_here, slab_tok, HS), jnp.float32),
    )
    key_piece = lax.all_gather(key_rows, "blk", axis=0, tiled=True)
    value_piece = lax.all_gather(val_rows, "blk", axis=0, tiled=True)
    key_count = key_piece.shape[0]
    block_len = min(1024, key_count)
    key_blocks = key_piece.reshape(key_count // block_len, block_len, heads_here, HS)
    value_blocks = value_piece.reshape(key_count // block_len, block_len, heads_here, HS)
    folded, unused = lax.scan(key_block, start_state, (key_blocks, value_blocks))
    running_max, running_sum, weighted = folded
    attended = (weighted / running_sum[:, :, None]).astype(jnp.bfloat16)
    head_rows = attended.transpose(1, 0, 2).reshape(slab_tok, heads_here * HS)
    partial = jnp.dot(head_rows, out_weight, preferred_element_type=jnp.float32)
    result = lax.psum_scatter(partial, "uly", scatter_dimension=0, tiled=True)
    return result.astype(jnp.bfloat16).reshape(z_count, x_count, y_count, features)


def solution(mesh):
    in_specs = (P("blk", None, "uly", None), P(), P(), P("uly", None), P("uly", None))
    out_specs = P("blk", None, "uly", None)
    return jax.shard_map(
        on_device, mesh=mesh, in_specs=in_specs, out_specs=out_specs, check_vma=False
    )
```

```python
import math

import jax
import jax.numpy as jnp
from jax import lax
from jax.sharding import PartitionSpec as P

HS = 64


def padded_2(shard, sides, width):
    for axis, dim in sides:
        size, length = (lax.axis_size(axis), shard.shape[dim])
        up = [(i, (i + 1) % size) for i in range(size - 1)]
        down = [(j, i) for i, j in up]
        last = lax.slice_in_dim(shard, length - width, length, axis=dim)
        initial = lax.slice_in_dim(shard, 0, width, axis=dim)
        before = lax.ppermute(last, axis, up)
        after = lax.ppermute(initial, axis, down)
        shard = jnp.concatenate([before, shard, after], axis=dim)
    return shard


def gathered(piece, axis):
    size = lax.axis_size(axis)
    parts = [piece]
    for shift in range(1, size):
        pairs = [(i, (i + shift) % size) for i in range(size)]
        parts.append(lax.ppermute(piece, axis, pairs))
    return jnp.concatenate(parts, axis=0)


def scattered_sum(whole, axis):
    size = lax.axis_size(axis)
    rank = lax.axis_index(axis)
    blocks = whole.reshape(size, whole.shape[0] // size, *whole.shape[1:])
    total = lax.dynamic_index_in_dim(blocks, rank, 0, keepdims=False)
    for shift in range(1, size):
        pairs = [(i, (i + shift) % size) for i in range(size)]
        outgoing = lax.dynamic_index_in_dim(blocks, (rank + shift) % size, 0, keepdims=False)
        total = total + lax.ppermute(outgoing, axis, pairs)
    return total


def times_transposed(left, right):
    return lax.dot_general(
        left, right, (((1,), (1,)), ((), ())), preferred_element_type=jnp.float32
    )


def on_device(tokens, conv_weight, conv_bias, qkv_weight, out_weight):
    z_count, x_count, y_count, features = tokens.shape
    padded = padded_2(tokens, (("blk", 0), ("uly", 2)), 1)
    padded = jnp.pad(padded, ((0, 0), (1, 1), (0, 0), (0, 0)))
    summed = tokens.astype(jnp.float32) + conv_bias
    for step_z in range(3):
        for step_x in range(3):
            for step_y in range(3):
                summed = (
                    summed
                    + conv_weight[9 * step_z + 3 * step_x + step_y]
                    * padded[
                        step_z : step_z + z_count,
                        step_x : step_x + x_count,
                        step_y : step_y + y_count,
                    ]
                )
    token_rows = summed.astype(jnp.bfloat16).reshape(-1, features)
    local_tok = token_rows.shape[0]
    heads_here = qkv_weight.shape[0] // (3 * HS)
    slab_rows = lax.all_gather(token_rows, "uly", axis=0, tiled=True)
    slab_tok = slab_rows.shape[0]
    projected = times_transposed(slab_rows, qkv_weight).astype(jnp.bfloat16)
    split_heads = projected.reshape(slab_tok, heads_here, 3, HS)
    queries = split_heads[:, :, 0]
    key_value = gathered(split_heads[:, :, 1:], "blk")
    key_piece = key_value[:, :, 0]
    value_piece = key_value[:, :, 1]
    score_scale = 1.0 / math.sqrt(HS)

    def key_block(carry_state, key_value):
        running_max, running_sum, weighted = carry_state
        key_part, value_part = key_value
        scores = (
            jnp.einsum("qhd,khd->hqk", queries, key_part, preferred_element_type=jnp.float32)
            * score_scale
        )
        new_max = jnp.maximum(running_max, jnp.max(scores, axis=2))
        shrink = jnp.exp(running_max - new_max)
        weights = jnp.exp(scores - new_max[:, :, None])
        running_sum = running_sum * shrink + jnp.sum(weights, axis=2)
        weighted = weighted * shrink[:, :, None] + jnp.einsum(
            "hqk,khd->hqd",
            weights.astype(jnp.bfloat16),
            value_part,
            preferred_element_type=jnp.float32,
        )
        return ((new_max, running_sum, weighted), None)

    start_state = (
        jnp.full((heads_here, slab_tok), -1e30, jnp.float32),
        jnp.zeros((heads_here, slab_tok), jnp.float32),
        jnp.zeros((heads_here, slab_tok, HS), jnp.float32),
    )
    key_count = key_piece.shape[0]
    block_len = min(1024, key_count)
    key_blocks = key_piece.reshape(key_count // block_len, block_len, heads_here, HS)
    value_blocks = value_piece.reshape(key_count // block_len, block_len, heads_here, HS)
    folded, unused = lax.scan(key_block, start_state, (key_blocks, value_blocks))
    running_max, running_sum, weighted = folded
    attended = (weighted / running_sum[:, :, None]).astype(jnp.bfloat16)
    head_rows = attended.transpose(1, 0, 2).reshape(slab_tok, heads_here * HS)
    partial = jnp.dot(head_rows, out_weight, preferred_element_type=jnp.float32)
    result = scattered_sum(partial, "uly")
    return result.astype(jnp.bfloat16).reshape(z_count, x_count, y_count, features)


def solution(mesh):
    in_specs = (P("blk", None, "uly", None), P(), P(), P("uly", None), P("uly", None))
    out_specs = P("blk", None, "uly", None)
    return jax.shard_map(
        on_device, mesh=mesh, in_specs=in_specs, out_specs=out_specs, check_vma=False
    )
```

```python
import math

import jax
import jax.numpy as jnp
from jax import lax
from jax.sharding import PartitionSpec as P

HS = 64


def padded_2(shard, sides, width):
    for axis, dim in sides:
        size, length = (lax.axis_size(axis), shard.shape[dim])
        up = [(i, (i + 1) % size) for i in range(size - 1)]
        down = [(j, i) for i, j in up]
        last = lax.slice_in_dim(shard, length - width, length, axis=dim)
        initial = lax.slice_in_dim(shard, 0, width, axis=dim)
        before = lax.ppermute(last, axis, up)
        after = lax.ppermute(initial, axis, down)
        shard = jnp.concatenate([before, shard, after], axis=dim)
    return shard


def gathered(piece, axis):
    size = lax.axis_size(axis)
    parts = [piece]
    for shift in range(1, size):
        pairs = [(i, (i + shift) % size) for i in range(size)]
        parts.append(lax.ppermute(piece, axis, pairs))
    return jnp.concatenate(parts, axis=0)


def scattered_sum(whole, axis):
    size = lax.axis_size(axis)
    rank = lax.axis_index(axis)
    blocks = whole.reshape(size, whole.shape[0] // size, *whole.shape[1:])
    total = lax.dynamic_index_in_dim(blocks, rank, 0, keepdims=False)
    for shift in range(1, size):
        pairs = [(i, (i + shift) % size) for i in range(size)]
        outgoing = lax.dynamic_index_in_dim(blocks, (rank + shift) % size, 0, keepdims=False)
        total = total + lax.ppermute(outgoing, axis, pairs)
    return total


def times_transposed(left, right):
    return lax.dot_general(
        left, right, (((1,), (1,)), ((), ())), preferred_element_type=jnp.float32
    )


def on_device(tokens, conv_weight, conv_bias, qkv_weight, out_weight):
    z_count, x_count, y_count, features = tokens.shape
    groups = lax.axis_size("uly")
    with_halo = padded_2(tokens, (("blk", 0),), 1)
    slab_in = lax.all_gather(with_halo, "uly", axis=0, tiled=False)
    slab_in = slab_in.transpose(1, 2, 0, 3, 4).reshape(
        z_count + 2, x_count, groups * y_count, features
    )
    slab_y = groups * y_count
    padded = jnp.pad(slab_in, ((0, 0), (1, 1), (1, 1), (0, 0)))
    summed = slab_in[1 : 1 + z_count].astype(jnp.float32) + conv_bias
    for step_z in range(3):
        for step_x in range(3):
            for step_y in range(3):
                summed = (
                    summed
                    + conv_weight[9 * step_z + 3 * step_x + step_y]
                    * padded[
                        step_z : step_z + z_count,
                        step_x : step_x + x_count,
                        step_y : step_y + slab_y,
                    ]
                )
    positioned = summed.astype(jnp.bfloat16)
    local_tok = z_count * x_count * y_count
    heads_here = qkv_weight.shape[0] // (3 * HS)
    slab_rows = (
        positioned.reshape(z_count, x_count, groups, y_count, features)
        .transpose(2, 0, 1, 3, 4)
        .reshape(groups * local_tok, features)
    )
    slab_tok = slab_rows.shape[0]
    projected = times_transposed(slab_rows, qkv_weight).astype(jnp.bfloat16)
    split_heads = projected.reshape(slab_tok, heads_here, 3, HS)
    queries = split_heads[:, :, 0]
    key_value = gathered(split_heads[:, :, 1:], "blk")
    key_piece = key_value[:, :, 0]
    value_piece = key_value[:, :, 1]
    score_scale = 1.0 / math.sqrt(HS)

    def key_block(carry_state, key_value):
        running_max, running_sum, weighted = carry_state
        key_part, value_part = key_value
        scores = (
            jnp.einsum("qhd,khd->hqk", queries, key_part, preferred_element_type=jnp.float32)
            * score_scale
        )
        new_max = jnp.maximum(running_max, jnp.max(scores, axis=2))
        shrink = jnp.exp(running_max - new_max)
        weights = jnp.exp(scores - new_max[:, :, None])
        running_sum = running_sum * shrink + jnp.sum(weights, axis=2)
        weighted = weighted * shrink[:, :, None] + jnp.einsum(
            "hqk,khd->hqd",
            weights.astype(jnp.bfloat16),
            value_part,
            preferred_element_type=jnp.float32,
        )
        return ((new_max, running_sum, weighted), None)

    start_state = (
        jnp.full((heads_here, slab_tok), -1e30, jnp.float32),
        jnp.zeros((heads_here, slab_tok), jnp.float32),
        jnp.zeros((heads_here, slab_tok, HS), jnp.float32),
    )
    key_count = key_piece.shape[0]
    block_len = min(1024, key_count)
    key_blocks = key_piece.reshape(key_count // block_len, block_len, heads_here, HS)
    value_blocks = value_piece.reshape(key_count // block_len, block_len, heads_here, HS)
    folded, unused = lax.scan(key_block, start_state, (key_blocks, value_blocks))
    running_max, running_sum, weighted = folded
    attended = (weighted / running_sum[:, :, None]).astype(jnp.bfloat16)
    head_rows = attended.transpose(1, 0, 2).reshape(slab_tok, heads_here * HS)
    partial = jnp.dot(head_rows, out_weight, preferred_element_type=jnp.float32)
    result = scattered_sum(partial, "uly")
    return result.astype(jnp.bfloat16).reshape(z_count, x_count, y_count, features)


def solution(mesh):
    in_specs = (P("blk", None, "uly", None), P(), P(), P("uly", None), P("uly", None))
    out_specs = P("blk", None, "uly", None)
    return jax.shard_map(
        on_device, mesh=mesh, in_specs=in_specs, out_specs=out_specs, check_vma=False
    )
```

```python
import math

import jax
import jax.numpy as jnp
from jax import lax
from jax.sharding import PartitionSpec as P

HS = 64


def padded_2(shard, sides, width):
    for axis, dim in sides:
        size, length = (lax.axis_size(axis), shard.shape[dim])
        up = [(i, (i + 1) % size) for i in range(size - 1)]
        down = [(j, i) for i, j in up]
        last = lax.slice_in_dim(shard, length - width, length, axis=dim)
        initial = lax.slice_in_dim(shard, 0, width, axis=dim)
        before = lax.ppermute(last, axis, up)
        after = lax.ppermute(initial, axis, down)
        shard = jnp.concatenate([before, shard, after], axis=dim)
    return shard


def gathered(piece, axis):
    size = lax.axis_size(axis)
    parts = [piece]
    for shift in range(1, size):
        pairs = [(i, (i + shift) % size) for i in range(size)]
        parts.append(lax.ppermute(piece, axis, pairs))
    return jnp.concatenate(parts, axis=0)


def relayed(piece, axis):
    size = lax.axis_size(axis)
    half = size // 2
    if size % 2:
        return gathered(piece, axis)
    mirror = [(i, (i + half) % size) for i in range(size)]
    crossed = lax.ppermute(piece, axis, mirror)
    parts = [piece, crossed]
    for shift in range(1, half):
        pairs = [(i, (i // half) * half + (i % half + shift) % half) for i in range(size)]
        parts.append(lax.ppermute(piece, axis, pairs))
        parts.append(lax.ppermute(crossed, axis, pairs))
    return jnp.concatenate(parts, axis=0)


def scattered_sum(whole, axis):
    size = lax.axis_size(axis)
    rank = lax.axis_index(axis)
    blocks = whole.reshape(size, whole.shape[0] // size, *whole.shape[1:])
    total = lax.dynamic_index_in_dim(blocks, rank, 0, keepdims=False)
    for shift in range(1, size):
        pairs = [(i, (i + shift) % size) for i in range(size)]
        outgoing = lax.dynamic_index_in_dim(blocks, (rank + shift) % size, 0, keepdims=False)
        total = total + lax.ppermute(outgoing, axis, pairs)
    return total


def times_transposed(left, right):
    return lax.dot_general(
        left, right, (((1,), (1,)), ((), ())), preferred_element_type=jnp.float32
    )


def on_device(tokens, conv_weight, conv_bias, qkv_weight, out_weight):
    z_count, x_count, y_count, features = tokens.shape
    groups = lax.axis_size("uly")
    with_halo = padded_2(tokens, (("blk", 0),), 1)
    slab_in = lax.all_gather(with_halo, "uly", axis=0, tiled=False)
    slab_in = slab_in.transpose(1, 2, 0, 3, 4).reshape(
        z_count + 2, x_count, groups * y_count, features
    )
    slab_y = groups * y_count
    padded = jnp.pad(slab_in, ((0, 0), (1, 1), (1, 1), (0, 0)))
    summed = slab_in[1 : 1 + z_count].astype(jnp.float32) + conv_bias
    for step_z in range(3):
        for step_x in range(3):
            for step_y in range(3):
                summed = (
                    summed
                    + conv_weight[9 * step_z + 3 * step_x + step_y]
                    * padded[
                        step_z : step_z + z_count,
                        step_x : step_x + x_count,
                        step_y : step_y + slab_y,
                    ]
                )
    positioned = summed.astype(jnp.bfloat16)
    local_tok = z_count * x_count * y_count
    heads_here = qkv_weight.shape[0] // (3 * HS)
    slab_rows = (
        positioned.reshape(z_count, x_count, groups, y_count, features)
        .transpose(2, 0, 1, 3, 4)
        .reshape(groups * local_tok, features)
    )
    slab_tok = slab_rows.shape[0]
    projected = times_transposed(slab_rows, qkv_weight).astype(jnp.bfloat16)
    split_heads = projected.reshape(slab_tok, heads_here, 3, HS)
    queries = split_heads[:, :, 0]
    key_value = relayed(split_heads[:, :, 1:], "blk")
    key_piece = key_value[:, :, 0]
    value_piece = key_value[:, :, 1]
    score_scale = 1.0 / math.sqrt(HS)

    def key_block(carry_state, key_value):
        running_max, running_sum, weighted = carry_state
        key_part, value_part = key_value
        scores = (
            jnp.einsum("qhd,khd->hqk", queries, key_part, preferred_element_type=jnp.float32)
            * score_scale
        )
        new_max = jnp.maximum(running_max, jnp.max(scores, axis=2))
        shrink = jnp.exp(running_max - new_max)
        weights = jnp.exp(scores - new_max[:, :, None])
        running_sum = running_sum * shrink + jnp.sum(weights, axis=2)
        weighted = weighted * shrink[:, :, None] + jnp.einsum(
            "hqk,khd->hqd",
            weights.astype(jnp.bfloat16),
            value_part,
            preferred_element_type=jnp.float32,
        )
        return ((new_max, running_sum, weighted), None)

    start_state = (
        jnp.full((heads_here, slab_tok), -1e30, jnp.float32),
        jnp.zeros((heads_here, slab_tok), jnp.float32),
        jnp.zeros((heads_here, slab_tok, HS), jnp.float32),
    )
    key_count = key_piece.shape[0]
    block_len = min(1024, key_count)
    key_blocks = key_piece.reshape(key_count // block_len, block_len, heads_here, HS)
    value_blocks = value_piece.reshape(key_count // block_len, block_len, heads_here, HS)
    folded, unused = lax.scan(key_block, start_state, (key_blocks, value_blocks))
    running_max, running_sum, weighted = folded
    attended = (weighted / running_sum[:, :, None]).astype(jnp.bfloat16)
    head_rows = attended.transpose(1, 0, 2).reshape(slab_tok, heads_here * HS)
    partial = jnp.dot(head_rows, out_weight, preferred_element_type=jnp.float32)
    result = scattered_sum(partial, "uly")
    return result.astype(jnp.bfloat16).reshape(z_count, x_count, y_count, features)


def solution(mesh):
    in_specs = (P("blk", None, "uly", None), P(), P(), P("uly", None), P("uly", None))
    out_specs = P("blk", None, "uly", None)
    return jax.shard_map(
        on_device, mesh=mesh, in_specs=in_specs, out_specs=out_specs, check_vma=False
    )
```

```python
import math

import jax
import jax.numpy as jnp
from jax import lax
from jax.sharding import PartitionSpec as P

HS = 64


def padded_2(shard, sides, width):
    for axis, dim in sides:
        size, length = (lax.axis_size(axis), shard.shape[dim])
        up = [(i, (i + 1) % size) for i in range(size - 1)]
        down = [(j, i) for i, j in up]
        last = lax.slice_in_dim(shard, length - width, length, axis=dim)
        initial = lax.slice_in_dim(shard, 0, width, axis=dim)
        before = lax.ppermute(last, axis, up)
        after = lax.ppermute(initial, axis, down)
        shard = jnp.concatenate([before, shard, after], axis=dim)
    return shard


def gathered(piece, axis):
    size = lax.axis_size(axis)
    parts = [piece]
    for shift in range(1, size):
        pairs = [(i, (i + shift) % size) for i in range(size)]
        parts.append(lax.ppermute(piece, axis, pairs))
    return jnp.concatenate(parts, axis=0)


def relayed(piece, axis):
    size = lax.axis_size(axis)
    half = size // 2
    if size % 2:
        return gathered(piece, axis)
    mirror = [(i, (i + half) % size) for i in range(size)]
    crossed = lax.ppermute(piece, axis, mirror)
    parts = [piece, crossed]
    for shift in range(1, half):
        pairs = [(i, (i // half) * half + (i % half + shift) % half) for i in range(size)]
        parts.append(lax.ppermute(piece, axis, pairs))
        parts.append(lax.ppermute(crossed, axis, pairs))
    return jnp.concatenate(parts, axis=0)


def chip_shift(size, shift):
    chips = size // 2
    return [(i, ((i // 2 + shift) % chips) * 2 + i % 2) for i in range(size)]


def gathered_by_chip(piece, axis):
    size = lax.axis_size(axis)
    rank = lax.axis_index(axis)
    chips, core = size // 2, rank % 2
    partner = [(i, i ^ 1) for i in range(size)]
    stacked = jnp.zeros((size,) + piece.shape, piece.dtype)
    stacked = lax.dynamic_update_index_in_dim(stacked, piece, rank, 0)
    near = lax.ppermute(piece, axis, partner)
    stacked = lax.dynamic_update_index_in_dim(stacked, near, rank ^ 1, 0)
    for shift in range(1, chips):
        source_chip = (rank // 2 - shift) % chips
        far = lax.ppermute(piece, axis, chip_shift(size, shift))
        stacked = lax.dynamic_update_index_in_dim(stacked, far, source_chip * 2 + core, 0)
        handed = lax.ppermute(far, axis, partner)
        stacked = lax.dynamic_update_index_in_dim(stacked, handed, source_chip * 2 + 1 - core, 0)
    return stacked


def scattered_sum_by_chip(whole, axis, shape):
    size = lax.axis_size(axis)
    rank = lax.axis_index(axis)
    chips, core, chip = size // 2, rank % 2, rank // 2
    blocks = whole.reshape(chips, 2, whole.shape[0] // size, *whole.shape[1:])
    mine = lax.dynamic_index_in_dim(blocks, core, 1, keepdims=False)
    theirs = lax.dynamic_index_in_dim(blocks, 1 - core, 1, keepdims=False)
    chip_sum = mine + lax.ppermute(theirs, axis, [(i, i ^ 1) for i in range(size)])
    total = lax.dynamic_index_in_dim(chip_sum, chip, 0, keepdims=False).reshape(shape)
    for shift in range(1, chips):
        outgoing = lax.dynamic_index_in_dim(chip_sum, (chip + shift) % chips, 0, keepdims=False)
        total = total + lax.ppermute(outgoing, axis, chip_shift(size, shift)).reshape(shape)
    return total


def scattered_sum(whole, axis):
    size = lax.axis_size(axis)
    rank = lax.axis_index(axis)
    blocks = whole.reshape(size, whole.shape[0] // size, *whole.shape[1:])
    total = lax.dynamic_index_in_dim(blocks, rank, 0, keepdims=False)
    for shift in range(1, size):
        pairs = [(i, (i + shift) % size) for i in range(size)]
        outgoing = lax.dynamic_index_in_dim(blocks, (rank + shift) % size, 0, keepdims=False)
        total = total + lax.ppermute(outgoing, axis, pairs)
    return total


def times_transposed(left, right):
    return lax.dot_general(
        left, right, (((1,), (1,)), ((), ())), preferred_element_type=jnp.float32
    )


def on_device(tokens, conv_weight, conv_bias, qkv_weight, out_weight):
    z_count, x_count, y_count, features = tokens.shape
    groups = lax.axis_size("uly")
    with_halo = padded_2(tokens, (("blk", 0),), 1)
    slab_in = gathered_by_chip(with_halo, "uly")
    slab_in = slab_in.transpose(1, 2, 0, 3, 4).reshape(
        z_count + 2, x_count, groups * y_count, features
    )
    slab_y = groups * y_count
    padded = jnp.pad(slab_in, ((0, 0), (1, 1), (1, 1), (0, 0)))
    summed = slab_in[1 : 1 + z_count].astype(jnp.float32) + conv_bias
    for step_z in range(3):
        for step_x in range(3):
            for step_y in range(3):
                summed = (
                    summed
                    + conv_weight[9 * step_z + 3 * step_x + step_y]
                    * padded[
                        step_z : step_z + z_count,
                        step_x : step_x + x_count,
                        step_y : step_y + slab_y,
                    ]
                )
    positioned = summed.astype(jnp.bfloat16)
    local_tok = z_count * x_count * y_count
    heads_here = qkv_weight.shape[0] // (3 * HS)
    slab_rows = (
        positioned.reshape(z_count, x_count, groups, y_count, features)
        .transpose(2, 0, 1, 3, 4)
        .reshape(groups * local_tok, features)
    )
    slab_tok = slab_rows.shape[0]
    projected = times_transposed(slab_rows, qkv_weight).astype(jnp.bfloat16)
    split_heads = projected.reshape(slab_tok, heads_here, 3, HS)
    queries = split_heads[:, :, 0]
    key_value = relayed(split_heads[:, :, 1:], "blk")
    key_piece = key_value[:, :, 0]
    value_piece = key_value[:, :, 1]
    score_scale = 1.0 / math.sqrt(HS)

    def key_block(carry_state, key_value):
        running_max, running_sum, weighted = carry_state
        key_part, value_part = key_value
        scores = (
            jnp.einsum("qhd,khd->hqk", queries, key_part, preferred_element_type=jnp.float32)
            * score_scale
        )
        new_max = jnp.maximum(running_max, jnp.max(scores, axis=2))
        shrink = jnp.exp(running_max - new_max)
        weights = jnp.exp(scores - new_max[:, :, None])
        running_sum = running_sum * shrink + jnp.sum(weights, axis=2)
        weighted = weighted * shrink[:, :, None] + jnp.einsum(
            "hqk,khd->hqd",
            weights.astype(jnp.bfloat16),
            value_part,
            preferred_element_type=jnp.float32,
        )
        return ((new_max, running_sum, weighted), None)

    start_state = (
        jnp.full((heads_here, slab_tok), -1e30, jnp.float32),
        jnp.zeros((heads_here, slab_tok), jnp.float32),
        jnp.zeros((heads_here, slab_tok, HS), jnp.float32),
    )
    key_count = key_piece.shape[0]
    block_len = min(1024, key_count)
    key_blocks = key_piece.reshape(key_count // block_len, block_len, heads_here, HS)
    value_blocks = value_piece.reshape(key_count // block_len, block_len, heads_here, HS)
    folded, unused = lax.scan(key_block, start_state, (key_blocks, value_blocks))
    running_max, running_sum, weighted = folded
    attended = (weighted / running_sum[:, :, None]).astype(jnp.bfloat16)
    head_rows = attended.transpose(1, 0, 2).reshape(slab_tok, heads_here * HS)
    partial = jnp.dot(head_rows, out_weight, preferred_element_type=jnp.float32)
    result = scattered_sum_by_chip(partial, "uly", tokens.shape)
    return result.astype(jnp.bfloat16)


def solution(mesh):
    in_specs = (P("blk", None, "uly", None), P(), P(), P("uly", None), P("uly", None))
    out_specs = P("blk", None, "uly", None)
    return jax.shard_map(
        on_device, mesh=mesh, in_specs=in_specs, out_specs=out_specs, check_vma=False
    )
```

```python
import math

import jax
import jax.numpy as jnp
from jax import lax
from jax.sharding import PartitionSpec as P

HS = 64


def padded_2(shard, sides, width):
    for axis, dim in sides:
        size, length = (lax.axis_size(axis), shard.shape[dim])
        up = [(i, (i + 1) % size) for i in range(size - 1)]
        down = [(j, i) for i, j in up]
        last = lax.slice_in_dim(shard, length - width, length, axis=dim)
        initial = lax.slice_in_dim(shard, 0, width, axis=dim)
        before = lax.ppermute(last, axis, up)
        after = lax.ppermute(initial, axis, down)
        shard = jnp.concatenate([before, shard, after], axis=dim)
    return shard


def gathered(piece, axis):
    size = lax.axis_size(axis)
    parts = [piece]
    for shift in range(1, size):
        pairs = [(i, (i + shift) % size) for i in range(size)]
        parts.append(lax.ppermute(piece, axis, pairs))
    return jnp.concatenate(parts, axis=0)


def relayed(piece, axis):
    size = lax.axis_size(axis)
    half = size // 2
    if size % 2:
        return gathered(piece, axis)
    mirror = [(i, (i + half) % size) for i in range(size)]
    crossed = lax.ppermute(piece, axis, mirror)
    parts = [piece, crossed]
    for shift in range(1, half):
        pairs = [(i, (i // half) * half + (i % half + shift) % half) for i in range(size)]
        parts.append(lax.ppermute(piece, axis, pairs))
        parts.append(lax.ppermute(crossed, axis, pairs))
    return jnp.concatenate(parts, axis=0)


def chip_shift(size, shift):
    chips = size // 2
    return [(i, ((i // 2 + shift) % chips) * 2 + i % 2) for i in range(size)]


def gathered_by_chip(piece, axis):
    size = lax.axis_size(axis)
    rank = lax.axis_index(axis)
    chips, core = size // 2, rank % 2
    partner = [(i, i ^ 1) for i in range(size)]
    stacked = jnp.zeros((size,) + piece.shape, piece.dtype)
    stacked = lax.dynamic_update_index_in_dim(stacked, piece, rank, 0)
    near = lax.ppermute(piece, axis, partner)
    stacked = lax.dynamic_update_index_in_dim(stacked, near, rank ^ 1, 0)
    for shift in range(1, chips):
        source_chip = (rank // 2 - shift) % chips
        far = lax.ppermute(piece, axis, chip_shift(size, shift))
        stacked = lax.dynamic_update_index_in_dim(stacked, far, source_chip * 2 + core, 0)
        handed = lax.ppermute(far, axis, partner)
        stacked = lax.dynamic_update_index_in_dim(stacked, handed, source_chip * 2 + 1 - core, 0)
    return stacked


def scattered_sum_by_chip(whole, axis, shape):
    size = lax.axis_size(axis)
    rank = lax.axis_index(axis)
    chips, core, chip = size // 2, rank % 2, rank // 2
    blocks = whole.reshape(chips, 2, whole.shape[0] // size, *whole.shape[1:])
    mine = lax.dynamic_index_in_dim(blocks, core, 1, keepdims=False)
    theirs = lax.dynamic_index_in_dim(blocks, 1 - core, 1, keepdims=False)
    chip_sum = mine + lax.ppermute(theirs, axis, [(i, i ^ 1) for i in range(size)])
    total = lax.dynamic_index_in_dim(chip_sum, chip, 0, keepdims=False).reshape(shape)
    for shift in range(1, chips):
        outgoing = lax.dynamic_index_in_dim(chip_sum, (chip + shift) % chips, 0, keepdims=False)
        arrived = lax.ppermute(outgoing.astype(jnp.bfloat16), axis, chip_shift(size, shift))
        total = total + arrived.astype(jnp.float32).reshape(shape)
    return total


def scattered_sum(whole, axis):
    size = lax.axis_size(axis)
    rank = lax.axis_index(axis)
    blocks = whole.reshape(size, whole.shape[0] // size, *whole.shape[1:])
    total = lax.dynamic_index_in_dim(blocks, rank, 0, keepdims=False)
    for shift in range(1, size):
        pairs = [(i, (i + shift) % size) for i in range(size)]
        outgoing = lax.dynamic_index_in_dim(blocks, (rank + shift) % size, 0, keepdims=False)
        total = total + lax.ppermute(outgoing, axis, pairs)
    return total


def times_transposed(left, right):
    return lax.dot_general(
        left, right, (((1,), (1,)), ((), ())), preferred_element_type=jnp.float32
    )


def on_device(tokens, conv_weight, conv_bias, qkv_weight, out_weight):
    z_count, x_count, y_count, features = tokens.shape
    groups = lax.axis_size("uly")
    with_halo = padded_2(tokens, (("blk", 0),), 1)
    slab_in = gathered_by_chip(with_halo, "uly")
    slab_in = slab_in.transpose(1, 2, 0, 3, 4).reshape(
        z_count + 2, x_count, groups * y_count, features
    )
    slab_y = groups * y_count
    padded = jnp.pad(slab_in, ((0, 0), (1, 1), (1, 1), (0, 0)))
    summed = slab_in[1 : 1 + z_count].astype(jnp.float32) + conv_bias
    for step_z in range(3):
        for step_x in range(3):
            for step_y in range(3):
                summed = (
                    summed
                    + conv_weight[9 * step_z + 3 * step_x + step_y]
                    * padded[
                        step_z : step_z + z_count,
                        step_x : step_x + x_count,
                        step_y : step_y + slab_y,
                    ]
                )
    positioned = summed.astype(jnp.bfloat16)
    local_tok = z_count * x_count * y_count
    heads_here = qkv_weight.shape[0] // (3 * HS)
    slab_rows = (
        positioned.reshape(z_count, x_count, groups, y_count, features)
        .transpose(2, 0, 1, 3, 4)
        .reshape(groups * local_tok, features)
    )
    slab_tok = slab_rows.shape[0]
    projected = times_transposed(slab_rows, qkv_weight).astype(jnp.bfloat16)
    split_heads = projected.reshape(slab_tok, heads_here, 3, HS)
    queries = split_heads[:, :, 0]
    key_value = relayed(split_heads[:, :, 1:], "blk")
    key_piece = key_value[:, :, 0]
    value_piece = key_value[:, :, 1]
    score_scale = 1.0 / math.sqrt(HS)

    def key_block(carry_state, key_value):
        running_max, running_sum, weighted = carry_state
        key_part, value_part = key_value
        scores = (
            jnp.einsum("qhd,khd->hqk", queries, key_part, preferred_element_type=jnp.float32)
            * score_scale
        )
        new_max = jnp.maximum(running_max, jnp.max(scores, axis=2))
        shrink = jnp.exp(running_max - new_max)
        weights = jnp.exp(scores - new_max[:, :, None])
        running_sum = running_sum * shrink + jnp.sum(weights, axis=2)
        weighted = weighted * shrink[:, :, None] + jnp.einsum(
            "hqk,khd->hqd",
            weights.astype(jnp.bfloat16),
            value_part,
            preferred_element_type=jnp.float32,
        )
        return ((new_max, running_sum, weighted), None)

    start_state = (
        jnp.full((heads_here, slab_tok), -1e30, jnp.float32),
        jnp.zeros((heads_here, slab_tok), jnp.float32),
        jnp.zeros((heads_here, slab_tok, HS), jnp.float32),
    )
    key_count = key_piece.shape[0]
    block_len = min(1024, key_count)
    key_blocks = key_piece.reshape(key_count // block_len, block_len, heads_here, HS)
    value_blocks = value_piece.reshape(key_count // block_len, block_len, heads_here, HS)
    folded, unused = lax.scan(key_block, start_state, (key_blocks, value_blocks))
    running_max, running_sum, weighted = folded
    attended = (weighted / running_sum[:, :, None]).astype(jnp.bfloat16)
    head_rows = attended.transpose(1, 0, 2).reshape(slab_tok, heads_here * HS)
    partial = jnp.dot(head_rows, out_weight, preferred_element_type=jnp.float32)
    result = scattered_sum_by_chip(partial, "uly", tokens.shape)
    return result.astype(jnp.bfloat16)


def solution(mesh):
    in_specs = (P("blk", None, "uly", None), P(), P(), P("uly", None), P("uly", None))
    out_specs = P("blk", None, "uly", None)
    return jax.shard_map(
        on_device, mesh=mesh, in_specs=in_specs, out_specs=out_specs, check_vma=False
    )
```

```python
import math

import jax
import jax.numpy as jnp
from jax import lax
from jax.sharding import PartitionSpec as P

HS = 64


def padded_2(shard, sides, width):
    for axis, dim in sides:
        size, length = (lax.axis_size(axis), shard.shape[dim])
        up = [(i, (i + 1) % size) for i in range(size - 1)]
        down = [(j, i) for i, j in up]
        last = lax.slice_in_dim(shard, length - width, length, axis=dim)
        initial = lax.slice_in_dim(shard, 0, width, axis=dim)
        before = lax.ppermute(last, axis, up)
        after = lax.ppermute(initial, axis, down)
        shard = jnp.concatenate([before, shard, after], axis=dim)
    return shard


def gathered(piece, axis):
    size = lax.axis_size(axis)
    parts = [piece]
    for shift in range(1, size):
        pairs = [(i, (i + shift) % size) for i in range(size)]
        parts.append(lax.ppermute(piece, axis, pairs))
    return jnp.concatenate(parts, axis=0)


def relayed(piece, axis):
    size = lax.axis_size(axis)
    half = size // 2
    if size % 2:
        return gathered(piece, axis)
    mirror = [(i, (i + half) % size) for i in range(size)]
    crossed = lax.ppermute(piece, axis, mirror)
    parts = [piece, crossed]
    for shift in range(1, half):
        pairs = [(i, (i // half) * half + (i % half + shift) % half) for i in range(size)]
        parts.append(lax.ppermute(piece, axis, pairs))
        parts.append(lax.ppermute(crossed, axis, pairs))
    return jnp.concatenate(parts, axis=0)


def chip_shift(size, shift):
    chips = size // 2
    return [(i, ((i // 2 + shift) % chips) * 2 + i % 2) for i in range(size)]


def gathered_by_chip(piece, axis):
    size = lax.axis_size(axis)
    rank = lax.axis_index(axis)
    chips, core = size // 2, rank % 2
    partner = [(i, i ^ 1) for i in range(size)]
    stacked = jnp.zeros((size,) + piece.shape, piece.dtype)
    stacked = lax.dynamic_update_index_in_dim(stacked, piece, rank, 0)
    near = lax.ppermute(piece, axis, partner)
    stacked = lax.dynamic_update_index_in_dim(stacked, near, rank ^ 1, 0)
    for shift in range(1, chips):
        source_chip = (rank // 2 - shift) % chips
        far = lax.ppermute(piece, axis, chip_shift(size, shift))
        stacked = lax.dynamic_update_index_in_dim(stacked, far, source_chip * 2 + core, 0)
        handed = lax.ppermute(far, axis, partner)
        stacked = lax.dynamic_update_index_in_dim(stacked, handed, source_chip * 2 + 1 - core, 0)
    return stacked


def scattered_sum_by_chip(whole, axis, shape):
    size = lax.axis_size(axis)
    rank = lax.axis_index(axis)
    chips, core, chip = size // 2, rank % 2, rank // 2
    blocks = whole.reshape(chips, 2, whole.shape[0] // size, *whole.shape[1:])
    mine = lax.dynamic_index_in_dim(blocks, core, 1, keepdims=False)
    theirs = lax.dynamic_index_in_dim(blocks, 1 - core, 1, keepdims=False)
    chip_sum = mine + lax.ppermute(theirs, axis, [(i, i ^ 1) for i in range(size)])
    total = lax.dynamic_index_in_dim(chip_sum, chip, 0, keepdims=False).reshape(shape)
    for shift in range(1, chips):
        outgoing = lax.dynamic_index_in_dim(chip_sum, (chip + shift) % chips, 0, keepdims=False)
        arrived = lax.ppermute(outgoing.astype(jnp.bfloat16), axis, chip_shift(size, shift))
        total = total + arrived.astype(jnp.float32).reshape(shape)
    return total


def scattered_sum(whole, axis):
    size = lax.axis_size(axis)
    rank = lax.axis_index(axis)
    blocks = whole.reshape(size, whole.shape[0] // size, *whole.shape[1:])
    total = lax.dynamic_index_in_dim(blocks, rank, 0, keepdims=False)
    for shift in range(1, size):
        pairs = [(i, (i + shift) % size) for i in range(size)]
        outgoing = lax.dynamic_index_in_dim(blocks, (rank + shift) % size, 0, keepdims=False)
        total = total + lax.ppermute(outgoing, axis, pairs)
    return total


def times_transposed(left, right):
    return lax.dot_general(
        left, right, (((1,), (1,)), ((), ())), preferred_element_type=jnp.float32
    )


def on_device(tokens, conv_weight, conv_bias, qkv_weight, out_weight):
    z_count, x_count, y_count, features = tokens.shape
    groups = lax.axis_size("uly")
    with_halo = padded_2(tokens, (("blk", 0),), 1)
    slab_in = gathered_by_chip(with_halo, "uly")
    slab_in = slab_in.transpose(1, 2, 0, 3, 4).reshape(
        z_count + 2, x_count, groups * y_count, features
    )
    slab_y = groups * y_count
    padded = jnp.pad(slab_in, ((0, 0), (1, 1), (1, 1), (0, 0)))
    summed = slab_in[1 : 1 + z_count].astype(jnp.float32) + conv_bias
    for step_z in range(3):
        for step_x in range(3):
            for step_y in range(3):
                summed = (
                    summed
                    + conv_weight[9 * step_z + 3 * step_x + step_y]
                    * padded[
                        step_z : step_z + z_count,
                        step_x : step_x + x_count,
                        step_y : step_y + slab_y,
                    ]
                )
    positioned = summed.astype(jnp.bfloat16)
    local_tok = z_count * x_count * y_count
    heads_here = qkv_weight.shape[0] // (3 * HS)
    slab_rows = (
        positioned.reshape(z_count, x_count, groups, y_count, features)
        .transpose(2, 0, 1, 3, 4)
        .reshape(groups * local_tok, features)
    )
    slab_tok = slab_rows.shape[0]
    projected = times_transposed(slab_rows, qkv_weight).astype(jnp.bfloat16)
    split_heads = projected.reshape(slab_tok, heads_here, 3, HS)
    queries = split_heads[:, :, 0]
    key_value = relayed(split_heads[:, :, 1:], "blk")
    key_piece = key_value[:, :, 0]
    value_piece = key_value[:, :, 1]
    score_scale = 1.0 / math.sqrt(HS)
    key_count = key_piece.shape[0]
    block_len = min(1024, key_count)
    key_blocks = key_piece.reshape(key_count // block_len, block_len, heads_here, HS)
    value_blocks = value_piece.reshape(key_count // block_len, block_len, heads_here, HS)

    def attend(query_rows):
        rows = query_rows.shape[0]

        def key_block(carry_state, key_value):
            running_max, running_sum, weighted = carry_state
            key_part, value_part = key_value
            scores = (
                jnp.einsum(
                    "qhd,khd->hqk", query_rows, key_part, preferred_element_type=jnp.float32
                )
                * score_scale
            )
            new_max = jnp.maximum(running_max, jnp.max(scores, axis=2))
            shrink = jnp.exp(running_max - new_max)
            weights = jnp.exp(scores - new_max[:, :, None])
            running_sum = running_sum * shrink + jnp.sum(weights, axis=2)
            weighted = weighted * shrink[:, :, None] + jnp.einsum(
                "hqk,khd->hqd",
                weights.astype(jnp.bfloat16),
                value_part,
                preferred_element_type=jnp.float32,
            )
            return ((new_max, running_sum, weighted), None)

        start_state = (
            jnp.full((heads_here, rows), -1e30, jnp.float32),
            jnp.zeros((heads_here, rows), jnp.float32),
            jnp.zeros((heads_here, rows, HS), jnp.float32),
        )
        folded, unused = lax.scan(key_block, start_state, (key_blocks, value_blocks))
        running_max, running_sum, weighted = folded
        attended = (weighted / running_sum[:, :, None]).astype(jnp.bfloat16)
        return attended.transpose(1, 0, 2).reshape(rows, heads_here * HS)

    rank = lax.axis_index("uly")
    chips, core, chip = groups // 2, rank % 2, rank // 2
    pair_queries = queries.reshape(chips, 2 * local_tok, heads_here, HS)
    total = None
    for shift in range(1, chips):
        far_rows = lax.dynamic_index_in_dim(pair_queries, (chip + shift) % chips, 0, keepdims=False)
        far_partial = jnp.dot(attend(far_rows), out_weight, preferred_element_type=jnp.float32)
        far_partial = far_partial.astype(jnp.bfloat16).reshape(2, local_tok, features)
        same_core = lax.dynamic_index_in_dim(far_partial, core, 0, keepdims=False)
        other_core = lax.dynamic_index_in_dim(far_partial, 1 - core, 0, keepdims=False)
        far_sent = (same_core, other_core)
        to_other_core = [
            (i, ((i // 2 + shift) % chips) * 2 + 1 - i % 2) for i in range(groups)
        ]
        for arrived in (
            lax.ppermute(same_core, "uly", chip_shift(groups, shift)),
            lax.ppermute(other_core, "uly", to_other_core),
        ):
            arrived = arrived.astype(jnp.float32).reshape(tokens.shape)
            total = arrived if total is None else total + arrived
    near_rows = lax.dynamic_index_in_dim(pair_queries, chip, 0, keepdims=False)
    if total is not None:
        near_rows, unused = lax.optimization_barrier((near_rows, far_sent))
    near_partial = jnp.dot(attend(near_rows), out_weight, preferred_element_type=jnp.float32)
    near_partial = near_partial.reshape(2, local_tok, features)
    own = lax.dynamic_index_in_dim(near_partial, core, 0, keepdims=False)
    for_partner = lax.dynamic_index_in_dim(near_partial, 1 - core, 0, keepdims=False)
    from_partner = lax.ppermute(for_partner, "uly", [(i, i ^ 1) for i in range(groups)])
    near_sum = own.reshape(tokens.shape) + from_partner.reshape(tokens.shape)
    result = near_sum if total is None else near_sum + total
    return result.astype(jnp.bfloat16)


def solution(mesh):
    in_specs = (P("blk", None, "uly", None), P(), P(), P("uly", None), P("uly", None))
    out_specs = P("blk", None, "uly", None)
    return jax.shard_map(
        on_device, mesh=mesh, in_specs=in_specs, out_specs=out_specs, check_vma=False
    )
```

```python
import math

import jax
import jax.numpy as jnp
from jax import lax
from jax.sharding import PartitionSpec as P

HS = 64


def padded_2(shard, sides, width):
    for axis, dim in sides:
        size, length = (lax.axis_size(axis), shard.shape[dim])
        up = [(i, (i + 1) % size) for i in range(size - 1)]
        down = [(j, i) for i, j in up]
        last = lax.slice_in_dim(shard, length - width, length, axis=dim)
        initial = lax.slice_in_dim(shard, 0, width, axis=dim)
        before = lax.ppermute(last, axis, up)
        after = lax.ppermute(initial, axis, down)
        shard = jnp.concatenate([before, shard, after], axis=dim)
    return shard


def gathered(piece, axis):
    size = lax.axis_size(axis)
    parts = [piece]
    for shift in range(1, size):
        pairs = [(i, (i + shift) % size) for i in range(size)]
        parts.append(lax.ppermute(piece, axis, pairs))
    return jnp.concatenate(parts, axis=0)


def relayed(piece, axis):
    size = lax.axis_size(axis)
    half = size // 2
    if size % 2:
        return gathered(piece, axis)
    mirror = [(i, (i + half) % size) for i in range(size)]
    crossed = lax.ppermute(piece, axis, mirror)
    parts = [piece, crossed]
    for shift in range(1, half):
        pairs = [(i, (i // half) * half + (i % half + shift) % half) for i in range(size)]
        parts.append(lax.ppermute(piece, axis, pairs))
        parts.append(lax.ppermute(crossed, axis, pairs))
    return jnp.concatenate(parts, axis=0)


def chip_shift(size, shift):
    chips = size // 2
    return [(i, ((i // 2 + shift) % chips) * 2 + i % 2) for i in range(size)]


def gathered_by_chip(piece, axis):
    size = lax.axis_size(axis)
    rank = lax.axis_index(axis)
    chips, core = size // 2, rank % 2
    partner = [(i, i ^ 1) for i in range(size)]
    stacked = jnp.zeros((size,) + piece.shape, piece.dtype)
    stacked = lax.dynamic_update_index_in_dim(stacked, piece, rank, 0)
    near = lax.ppermute(piece, axis, partner)
    stacked = lax.dynamic_update_index_in_dim(stacked, near, rank ^ 1, 0)
    for shift in range(1, chips):
        source_chip = (rank // 2 - shift) % chips
        far = lax.ppermute(piece, axis, chip_shift(size, shift))
        stacked = lax.dynamic_update_index_in_dim(stacked, far, source_chip * 2 + core, 0)
        handed = lax.ppermute(far, axis, partner)
        stacked = lax.dynamic_update_index_in_dim(stacked, handed, source_chip * 2 + 1 - core, 0)
    return stacked


def scattered_sum_by_chip(whole, axis, shape):
    size = lax.axis_size(axis)
    rank = lax.axis_index(axis)
    chips, core, chip = size // 2, rank % 2, rank // 2
    blocks = whole.reshape(chips, 2, whole.shape[0] // size, *whole.shape[1:])
    mine = lax.dynamic_index_in_dim(blocks, core, 1, keepdims=False)
    theirs = lax.dynamic_index_in_dim(blocks, 1 - core, 1, keepdims=False)
    chip_sum = mine + lax.ppermute(theirs, axis, [(i, i ^ 1) for i in range(size)])
    total = lax.dynamic_index_in_dim(chip_sum, chip, 0, keepdims=False).reshape(shape)
    for shift in range(1, chips):
        outgoing = lax.dynamic_index_in_dim(chip_sum, (chip + shift) % chips, 0, keepdims=False)
        arrived = lax.ppermute(outgoing.astype(jnp.bfloat16), axis, chip_shift(size, shift))
        total = total + arrived.astype(jnp.float32).reshape(shape)
    return total


def scattered_sum(whole, axis):
    size = lax.axis_size(axis)
    rank = lax.axis_index(axis)
    blocks = whole.reshape(size, whole.shape[0] // size, *whole.shape[1:])
    total = lax.dynamic_index_in_dim(blocks, rank, 0, keepdims=False)
    for shift in range(1, size):
        pairs = [(i, (i + shift) % size) for i in range(size)]
        outgoing = lax.dynamic_index_in_dim(blocks, (rank + shift) % size, 0, keepdims=False)
        total = total + lax.ppermute(outgoing, axis, pairs)
    return total


def times_transposed(left, right):
    return lax.dot_general(
        left, right, (((1,), (1,)), ((), ())), preferred_element_type=jnp.float32
    )


def on_device(tokens, conv_weight, conv_bias, qkv_weight, out_weight):
    z_count, x_count, y_count, features = tokens.shape
    groups = lax.axis_size("uly")
    with_halo = padded_2(tokens, (("blk", 0),), 1)
    slab_in = gathered_by_chip(with_halo, "uly")
    slab_in = slab_in.transpose(1, 2, 0, 3, 4).reshape(
        z_count + 2, x_count, groups * y_count, features
    )
    slab_y = groups * y_count
    padded = jnp.pad(slab_in, ((0, 0), (1, 1), (1, 1), (0, 0)))
    summed = slab_in[1 : 1 + z_count].astype(jnp.float32) + conv_bias
    for step_z in range(3):
        for step_x in range(3):
            for step_y in range(3):
                summed = (
                    summed
                    + conv_weight[9 * step_z + 3 * step_x + step_y]
                    * padded[
                        step_z : step_z + z_count,
                        step_x : step_x + x_count,
                        step_y : step_y + slab_y,
                    ]
                )
    positioned = summed.astype(jnp.bfloat16)
    local_tok = z_count * x_count * y_count
    heads_here = qkv_weight.shape[0] // (3 * HS)
    slab_rows = (
        positioned.reshape(z_count, x_count, groups, y_count, features)
        .transpose(2, 0, 1, 3, 4)
        .reshape(groups * local_tok, features)
    )
    slab_tok = slab_rows.shape[0]
    projected = times_transposed(slab_rows, qkv_weight).astype(jnp.bfloat16)
    split_heads = projected.reshape(slab_tok, heads_here, 3, HS)
    queries = split_heads[:, :, 0]
    key_value = relayed(split_heads[:, :, 1:], "blk")
    key_piece = key_value[:, :, 0]
    value_piece = key_value[:, :, 1]
    score_scale = 1.0 / math.sqrt(HS)
    key_count = key_piece.shape[0]
    block_len = min(1024, key_count)
    key_blocks = key_piece.reshape(key_count // block_len, block_len, heads_here, HS)
    value_blocks = value_piece.reshape(key_count // block_len, block_len, heads_here, HS)

    def attend(query_rows):
        rows = query_rows.shape[0]

        def key_block(carry_state, key_value):
            running_max, running_sum, weighted = carry_state
            key_part, value_part = key_value
            scores = (
                jnp.einsum(
                    "qhd,khd->hqk", query_rows, key_part, preferred_element_type=jnp.float32
                )
                * score_scale
            )
            new_max = jnp.maximum(running_max, jnp.max(scores, axis=2))
            shrink = jnp.exp(running_max - new_max)
            weights = jnp.exp(scores - new_max[:, :, None])
            running_sum = running_sum * shrink + jnp.sum(weights, axis=2)
            weighted = weighted * shrink[:, :, None] + jnp.einsum(
                "hqk,khd->hqd",
                weights.astype(jnp.bfloat16),
                value_part,
                preferred_element_type=jnp.float32,
            )
            return ((new_max, running_sum, weighted), None)

        start_state = (
            jnp.full((heads_here, rows), -1e30, jnp.float32),
            jnp.zeros((heads_here, rows), jnp.float32),
            jnp.zeros((heads_here, rows, HS), jnp.float32),
        )
        folded, unused = lax.scan(key_block, start_state, (key_blocks, value_blocks))
        running_max, running_sum, weighted = folded
        attended = (weighted / running_sum[:, :, None]).astype(jnp.bfloat16)
        return attended.transpose(1, 0, 2).reshape(rows, heads_here * HS)

    rank = lax.axis_index("uly")
    chips, core, chip = groups // 2, rank % 2, rank // 2
    rank_queries = queries.reshape(groups, local_tok, heads_here, HS)
    partner = [(i, i ^ 1) for i in range(groups)]
    plan = []
    for shift in range(1, chips):
        to_other_core = [
            (i, ((i // 2 + shift) % chips) * 2 + 1 - i % 2) for i in range(groups)
        ]
        target_chip = (chip + shift) % chips
        plan.append((target_chip * 2 + core, chip_shift(groups, shift), jnp.bfloat16))
        plan.append((target_chip * 2 + 1 - core, to_other_core, jnp.bfloat16))
    plan.append((rank ^ 1, partner, jnp.float32))
    total = None
    sent = None
    for target, pairs, link_type in plan:
        rows = lax.dynamic_index_in_dim(rank_queries, target, 0, keepdims=False)
        if sent is not None:
            rows, unused = lax.optimization_barrier((rows, sent))
        part = jnp.dot(attend(rows), out_weight, preferred_element_type=jnp.float32)
        sent = part.astype(link_type)
        arrived = lax.ppermute(sent, "uly", pairs).astype(jnp.float32).reshape(tokens.shape)
        total = arrived if total is None else total + arrived
    rows = lax.dynamic_index_in_dim(rank_queries, rank, 0, keepdims=False)
    rows, unused = lax.optimization_barrier((rows, sent))
    own = jnp.dot(attend(rows), out_weight, preferred_element_type=jnp.float32)
    result = own.reshape(tokens.shape) + total
    return result.astype(jnp.bfloat16)


def solution(mesh):
    in_specs = (P("blk", None, "uly", None), P(), P(), P("uly", None), P("uly", None))
    out_specs = P("blk", None, "uly", None)
    return jax.shard_map(
        on_device, mesh=mesh, in_specs=in_specs, out_specs=out_specs, check_vma=False
    )
```

```python
import math

import jax
import jax.numpy as jnp
from jax import lax
from jax.sharding import PartitionSpec as P

HS = 64


def padded_2(shard, sides, width):
    for axis, dim in sides:
        size, length = (lax.axis_size(axis), shard.shape[dim])
        up = [(i, (i + 1) % size) for i in range(size - 1)]
        down = [(j, i) for i, j in up]
        last = lax.slice_in_dim(shard, length - width, length, axis=dim)
        initial = lax.slice_in_dim(shard, 0, width, axis=dim)
        before = lax.ppermute(last, axis, up)
        after = lax.ppermute(initial, axis, down)
        shard = jnp.concatenate([before, shard, after], axis=dim)
    return shard


def gathered(piece, axis):
    size = lax.axis_size(axis)
    parts = [piece]
    for shift in range(1, size):
        pairs = [(i, (i + shift) % size) for i in range(size)]
        parts.append(lax.ppermute(piece, axis, pairs))
    return jnp.concatenate(parts, axis=0)


def relayed(piece, axis):
    size = lax.axis_size(axis)
    half = size // 2
    if size % 2:
        return gathered(piece, axis)
    mirror = [(i, (i + half) % size) for i in range(size)]
    crossed = lax.ppermute(piece, axis, mirror)
    parts = [piece, crossed]
    for shift in range(1, half):
        pairs = [(i, (i // half) * half + (i % half + shift) % half) for i in range(size)]
        parts.append(lax.ppermute(piece, axis, pairs))
        parts.append(lax.ppermute(crossed, axis, pairs))
    return jnp.concatenate(parts, axis=0)


def chip_shift(size, shift):
    chips = size // 2
    return [(i, ((i // 2 + shift) % chips) * 2 + i % 2) for i in range(size)]


def gathered_by_chip(piece, axis):
    size = lax.axis_size(axis)
    rank = lax.axis_index(axis)
    chips, core = size // 2, rank % 2
    partner = [(i, i ^ 1) for i in range(size)]
    stacked = jnp.zeros((size,) + piece.shape, piece.dtype)
    stacked = lax.dynamic_update_index_in_dim(stacked, piece, rank, 0)
    near = lax.ppermute(piece, axis, partner)
    stacked = lax.dynamic_update_index_in_dim(stacked, near, rank ^ 1, 0)
    for shift in range(1, chips):
        source_chip = (rank // 2 - shift) % chips
        far = lax.ppermute(piece, axis, chip_shift(size, shift))
        stacked = lax.dynamic_update_index_in_dim(stacked, far, source_chip * 2 + core, 0)
        handed = lax.ppermute(far, axis, partner)
        stacked = lax.dynamic_update_index_in_dim(stacked, handed, source_chip * 2 + 1 - core, 0)
    return stacked


def scattered_sum_by_chip(whole, axis, shape):
    size = lax.axis_size(axis)
    rank = lax.axis_index(axis)
    chips, core, chip = size // 2, rank % 2, rank // 2
    blocks = whole.reshape(chips, 2, whole.shape[0] // size, *whole.shape[1:])
    mine = lax.dynamic_index_in_dim(blocks, core, 1, keepdims=False)
    theirs = lax.dynamic_index_in_dim(blocks, 1 - core, 1, keepdims=False)
    chip_sum = mine + lax.ppermute(theirs, axis, [(i, i ^ 1) for i in range(size)])
    total = lax.dynamic_index_in_dim(chip_sum, chip, 0, keepdims=False).reshape(shape)
    for shift in range(1, chips):
        outgoing = lax.dynamic_index_in_dim(chip_sum, (chip + shift) % chips, 0, keepdims=False)
        arrived = lax.ppermute(outgoing.astype(jnp.bfloat16), axis, chip_shift(size, shift))
        total = total + arrived.astype(jnp.float32).reshape(shape)
    return total


def scattered_sum(whole, axis):
    size = lax.axis_size(axis)
    rank = lax.axis_index(axis)
    blocks = whole.reshape(size, whole.shape[0] // size, *whole.shape[1:])
    total = lax.dynamic_index_in_dim(blocks, rank, 0, keepdims=False)
    for shift in range(1, size):
        pairs = [(i, (i + shift) % size) for i in range(size)]
        outgoing = lax.dynamic_index_in_dim(blocks, (rank + shift) % size, 0, keepdims=False)
        total = total + lax.ppermute(outgoing, axis, pairs)
    return total


def times_transposed(left, right):
    return lax.dot_general(
        left, right, (((1,), (1,)), ((), ())), preferred_element_type=jnp.float32
    )


def on_device(tokens, conv_weight, conv_bias, qkv_weight, out_weight):
    z_count, x_count, y_count, features = tokens.shape
    groups = lax.axis_size("uly")
    with_halo = padded_2(tokens, (("blk", 0),), 1)
    slab_in = gathered_by_chip(with_halo, "uly")
    slab_in = slab_in.transpose(1, 2, 0, 3, 4).reshape(
        z_count + 2, x_count, groups * y_count, features
    )
    slab_y = groups * y_count
    padded = jnp.pad(slab_in, ((0, 0), (1, 1), (1, 1), (0, 0)))
    summed = slab_in[1 : 1 + z_count].astype(jnp.float32) + conv_bias
    for step_z in range(3):
        for step_x in range(3):
            for step_y in range(3):
                summed = (
                    summed
                    + conv_weight[9 * step_z + 3 * step_x + step_y]
                    * padded[
                        step_z : step_z + z_count,
                        step_x : step_x + x_count,
                        step_y : step_y + slab_y,
                    ]
                )
    positioned = summed.astype(jnp.bfloat16)
    local_tok = z_count * x_count * y_count
    heads_here = qkv_weight.shape[0] // (3 * HS)
    slab_rows = positioned.reshape(-1, features)
    slab_tok = slab_rows.shape[0]
    projected = times_transposed(slab_rows, qkv_weight).astype(jnp.bfloat16)
    split_heads = projected.reshape(slab_tok, heads_here, 3, HS)
    queries = split_heads[:, :, 0]
    key_value = relayed(split_heads[:, :, 1:], "blk")
    key_piece = key_value[:, :, 0]
    value_piece = key_value[:, :, 1]
    score_scale = 1.0 / math.sqrt(HS)
    key_count = key_piece.shape[0]
    block_len = min(1024, key_count)
    key_blocks = key_piece.reshape(key_count // block_len, block_len, heads_here, HS)
    value_blocks = value_piece.reshape(key_count // block_len, block_len, heads_here, HS)

    def attend(query_rows):
        rows = query_rows.shape[0]

        def key_block(carry_state, key_value):
            running_max, running_sum, weighted = carry_state
            key_part, value_part = key_value
            scores = (
                jnp.einsum(
                    "qhd,khd->hqk", query_rows, key_part, preferred_element_type=jnp.float32
                )
                * score_scale
            )
            new_max = jnp.maximum(running_max, jnp.max(scores, axis=2))
            shrink = jnp.exp(running_max - new_max)
            weights = jnp.exp(scores - new_max[:, :, None])
            running_sum = running_sum * shrink + jnp.sum(weights, axis=2)
            weighted = weighted * shrink[:, :, None] + jnp.einsum(
                "hqk,khd->hqd",
                weights.astype(jnp.bfloat16),
                value_part,
                preferred_element_type=jnp.float32,
            )
            return ((new_max, running_sum, weighted), None)

        start_state = (
            jnp.full((heads_here, rows), -1e30, jnp.float32),
            jnp.zeros((heads_here, rows), jnp.float32),
            jnp.zeros((heads_here, rows, HS), jnp.float32),
        )
        folded, unused = lax.scan(key_block, start_state, (key_blocks, value_blocks))
        running_max, running_sum, weighted = folded
        attended = (weighted / running_sum[:, :, None]).astype(jnp.bfloat16)
        return attended.transpose(1, 0, 2).reshape(rows, heads_here * HS)

    rank = lax.axis_index("uly")
    chips, core, chip = groups // 2, rank % 2, rank // 2
    pair_queries = queries.reshape(z_count, x_count, chips, 2 * y_count, heads_here, HS)

    def rows_of_chip(which):
        picked = lax.dynamic_index_in_dim(pair_queries, which, 2, keepdims=False)
        return picked.reshape(2 * local_tok, heads_here, HS)

    def split_by_core(partial):
        return partial.reshape(z_count, x_count, 2, y_count, features)
    total = None
    for shift in range(1, chips):
        far_rows = rows_of_chip((chip + shift) % chips)
        far_partial = jnp.dot(attend(far_rows), out_weight, preferred_element_type=jnp.float32)
        far_partial = split_by_core(far_partial.astype(jnp.bfloat16))
        same_core = lax.dynamic_index_in_dim(far_partial, core, 2, keepdims=False)
        other_core = lax.dynamic_index_in_dim(far_partial, 1 - core, 2, keepdims=False)
        far_sent = (same_core, other_core)
        to_other_core = [
            (i, ((i // 2 + shift) % chips) * 2 + 1 - i % 2) for i in range(groups)
        ]
        for arrived in (
            lax.ppermute(same_core, "uly", chip_shift(groups, shift)),
            lax.ppermute(other_core, "uly", to_other_core),
        ):
            arrived = arrived.astype(jnp.float32)
            total = arrived if total is None else total + arrived
    near_rows = rows_of_chip(chip)
    if total is not None:
        near_rows, unused = lax.optimization_barrier((near_rows, far_sent))
    near_partial = jnp.dot(attend(near_rows), out_weight, preferred_element_type=jnp.float32)
    near_partial = split_by_core(near_partial)
    own = lax.dynamic_index_in_dim(near_partial, core, 2, keepdims=False)
    for_partner = lax.dynamic_index_in_dim(near_partial, 1 - core, 2, keepdims=False)
    from_partner = lax.ppermute(for_partner, "uly", [(i, i ^ 1) for i in range(groups)])
    near_sum = own + from_partner
    result = near_sum if total is None else near_sum + total
    return result.astype(jnp.bfloat16)


def solution(mesh):
    in_specs = (P("blk", None, "uly", None), P(), P(), P("uly", None), P("uly", None))
    out_specs = P("blk", None, "uly", None)
    return jax.shard_map(
        on_device, mesh=mesh, in_specs=in_specs, out_specs=out_specs, check_vma=False
    )
```

```python
import math

import jax
import jax.numpy as jnp
from jax import lax
from jax.sharding import PartitionSpec as P

HS = 64


def padded_2(shard, sides, width):
    for axis, dim in sides:
        size, length = (lax.axis_size(axis), shard.shape[dim])
        up = [(i, (i + 1) % size) for i in range(size - 1)]
        down = [(j, i) for i, j in up]
        last = lax.slice_in_dim(shard, length - width, length, axis=dim)
        initial = lax.slice_in_dim(shard, 0, width, axis=dim)
        before = lax.ppermute(last, axis, up)
        after = lax.ppermute(initial, axis, down)
        shard = jnp.concatenate([before, shard, after], axis=dim)
    return shard


def gathered(piece, axis):
    size = lax.axis_size(axis)
    parts = [piece]
    for shift in range(1, size):
        pairs = [(i, (i + shift) % size) for i in range(size)]
        parts.append(lax.ppermute(piece, axis, pairs))
    return jnp.concatenate(parts, axis=0)


def relayed(piece, axis):
    size = lax.axis_size(axis)
    half = size // 2
    if size % 2:
        return gathered(piece, axis)
    mirror = [(i, (i + half) % size) for i in range(size)]
    crossed = lax.ppermute(piece, axis, mirror)
    parts = [piece, crossed]
    for shift in range(1, half):
        pairs = [(i, (i // half) * half + (i % half + shift) % half) for i in range(size)]
        parts.append(lax.ppermute(piece, axis, pairs))
        parts.append(lax.ppermute(crossed, axis, pairs))
    return jnp.concatenate(parts, axis=0)


def chip_shift(size, shift):
    chips = size // 2
    return [(i, ((i // 2 + shift) % chips) * 2 + i % 2) for i in range(size)]


def gathered_by_chip(piece, axis):
    size = lax.axis_size(axis)
    rank = lax.axis_index(axis)
    chips, core = size // 2, rank % 2
    partner = [(i, i ^ 1) for i in range(size)]
    stacked = jnp.zeros((size,) + piece.shape, piece.dtype)
    stacked = lax.dynamic_update_index_in_dim(stacked, piece, rank, 0)
    near = lax.ppermute(piece, axis, partner)
    stacked = lax.dynamic_update_index_in_dim(stacked, near, rank ^ 1, 0)
    for shift in range(1, chips):
        source_chip = (rank // 2 - shift) % chips
        far = lax.ppermute(piece, axis, chip_shift(size, shift))
        stacked = lax.dynamic_update_index_in_dim(stacked, far, source_chip * 2 + core, 0)
        handed = lax.ppermute(far, axis, partner)
        stacked = lax.dynamic_update_index_in_dim(stacked, handed, source_chip * 2 + 1 - core, 0)
    return stacked


def scattered_sum_by_chip(whole, axis, shape):
    size = lax.axis_size(axis)
    rank = lax.axis_index(axis)
    chips, core, chip = size // 2, rank % 2, rank // 2
    blocks = whole.reshape(chips, 2, whole.shape[0] // size, *whole.shape[1:])
    mine = lax.dynamic_index_in_dim(blocks, core, 1, keepdims=False)
    theirs = lax.dynamic_index_in_dim(blocks, 1 - core, 1, keepdims=False)
    chip_sum = mine + lax.ppermute(theirs, axis, [(i, i ^ 1) for i in range(size)])
    total = lax.dynamic_index_in_dim(chip_sum, chip, 0, keepdims=False).reshape(shape)
    for shift in range(1, chips):
        outgoing = lax.dynamic_index_in_dim(chip_sum, (chip + shift) % chips, 0, keepdims=False)
        arrived = lax.ppermute(outgoing.astype(jnp.bfloat16), axis, chip_shift(size, shift))
        total = total + arrived.astype(jnp.float32).reshape(shape)
    return total


def scattered_sum(whole, axis):
    size = lax.axis_size(axis)
    rank = lax.axis_index(axis)
    blocks = whole.reshape(size, whole.shape[0] // size, *whole.shape[1:])
    total = lax.dynamic_index_in_dim(blocks, rank, 0, keepdims=False)
    for shift in range(1, size):
        pairs = [(i, (i + shift) % size) for i in range(size)]
        outgoing = lax.dynamic_index_in_dim(blocks, (rank + shift) % size, 0, keepdims=False)
        total = total + lax.ppermute(outgoing, axis, pairs)
    return total


def times_transposed(left, right):
    return lax.dot_general(
        left, right, (((1,), (1,)), ((), ())), preferred_element_type=jnp.float32
    )


def on_device(tokens, conv_weight, conv_bias, qkv_weight, out_weight):
    z_count, x_count, y_count, features = tokens.shape
    groups = lax.axis_size("uly")
    with_halo = padded_2(tokens, (("blk", 0),), 1)
    slab_in = gathered_by_chip(with_halo, "uly")
    lanes = 128 if features % 128 == 0 else features
    tile_shape = (features // lanes, lanes)
    slab_in = slab_in.transpose(1, 2, 0, 3, 4).reshape(
        z_count + 2, x_count, groups * y_count, *tile_shape
    )
    slab_y = groups * y_count
    padded = jnp.pad(slab_in, ((0, 0), (1, 1), (1, 1), (0, 0), (0, 0)))
    tap_weight = conv_weight.reshape(27, *tile_shape)
    summed = slab_in[1 : 1 + z_count].astype(jnp.float32) + conv_bias.reshape(tile_shape)
    for step_z in range(3):
        for step_x in range(3):
            for step_y in range(3):
                summed = (
                    summed
                    + tap_weight[9 * step_z + 3 * step_x + step_y]
                    * padded[
                        step_z : step_z + z_count,
                        step_x : step_x + x_count,
                        step_y : step_y + slab_y,
                    ]
                )
    summed = summed.reshape(z_count, x_count, slab_y, features)
    positioned = summed.astype(jnp.bfloat16)
    local_tok = z_count * x_count * y_count
    heads_here = qkv_weight.shape[0] // (3 * HS)
    slab_rows = (
        positioned.reshape(z_count, x_count, groups, y_count, features)
        .transpose(2, 0, 1, 3, 4)
        .reshape(groups * local_tok, features)
    )
    slab_tok = slab_rows.shape[0]
    projected = times_transposed(slab_rows, qkv_weight).astype(jnp.bfloat16)
    split_heads = projected.reshape(slab_tok, heads_here, 3, HS)
    queries = split_heads[:, :, 0]
    key_value = relayed(split_heads[:, :, 1:], "blk")
    key_piece = key_value[:, :, 0]
    value_piece = key_value[:, :, 1]
    score_scale = 1.0 / math.sqrt(HS)
    key_count = key_piece.shape[0]
    block_len = min(1024, key_count)
    key_blocks = key_piece.reshape(key_count // block_len, block_len, heads_here, HS)
    value_blocks = value_piece.reshape(key_count // block_len, block_len, heads_here, HS)

    def attend(query_rows):
        rows = query_rows.shape[0]

        def key_block(carry_state, key_value):
            running_max, running_sum, weighted = carry_state
            key_part, value_part = key_value
            scores = (
                jnp.einsum(
                    "qhd,khd->hqk", query_rows, key_part, preferred_element_type=jnp.float32
                )
                * score_scale
            )
            new_max = jnp.maximum(running_max, jnp.max(scores, axis=2))
            shrink = jnp.exp(running_max - new_max)
            weights = jnp.exp(scores - new_max[:, :, None])
            running_sum = running_sum * shrink + jnp.sum(weights, axis=2)
            weighted = weighted * shrink[:, :, None] + jnp.einsum(
                "hqk,khd->hqd",
                weights.astype(jnp.bfloat16),
                value_part,
                preferred_element_type=jnp.float32,
            )
            return ((new_max, running_sum, weighted), None)

        start_state = (
            jnp.full((heads_here, rows), -1e30, jnp.float32),
            jnp.zeros((heads_here, rows), jnp.float32),
            jnp.zeros((heads_here, rows, HS), jnp.float32),
        )
        folded, unused = lax.scan(key_block, start_state, (key_blocks, value_blocks))
        running_max, running_sum, weighted = folded
        attended = (weighted / running_sum[:, :, None]).astype(jnp.bfloat16)
        return attended.transpose(1, 0, 2).reshape(rows, heads_here * HS)

    rank = lax.axis_index("uly")
    chips, core, chip = groups // 2, rank % 2, rank // 2
    pair_queries = queries.reshape(chips, 2 * local_tok, heads_here, HS)
    total = None
    for shift in range(1, chips):
        far_rows = lax.dynamic_index_in_dim(pair_queries, (chip + shift) % chips, 0, keepdims=False)
        far_partial = jnp.dot(attend(far_rows), out_weight, preferred_element_type=jnp.float32)
        far_partial = far_partial.astype(jnp.bfloat16).reshape(2, local_tok, features)
        same_core = lax.dynamic_index_in_dim(far_partial, core, 0, keepdims=False)
        other_core = lax.dynamic_index_in_dim(far_partial, 1 - core, 0, keepdims=False)
        far_sent = (same_core, other_core)
        to_other_core = [
            (i, ((i // 2 + shift) % chips) * 2 + 1 - i % 2) for i in range(groups)
        ]
        for arrived in (
            lax.ppermute(same_core, "uly", chip_shift(groups, shift)),
            lax.ppermute(other_core, "uly", to_other_core),
        ):
            arrived = arrived.astype(jnp.float32).reshape(tokens.shape)
            total = arrived if total is None else total + arrived
    near_rows = lax.dynamic_index_in_dim(pair_queries, chip, 0, keepdims=False)
    if total is not None:
        near_rows, unused = lax.optimization_barrier((near_rows, far_sent))
    near_partial = jnp.dot(attend(near_rows), out_weight, preferred_element_type=jnp.float32)
    near_partial = near_partial.reshape(2, local_tok, features)
    own = lax.dynamic_index_in_dim(near_partial, core, 0, keepdims=False)
    for_partner = lax.dynamic_index_in_dim(near_partial, 1 - core, 0, keepdims=False)
    from_partner = lax.ppermute(for_partner, "uly", [(i, i ^ 1) for i in range(groups)])
    near_sum = own.reshape(tokens.shape) + from_partner.reshape(tokens.shape)
    result = near_sum if total is None else near_sum + total
    return result.astype(jnp.bfloat16)


def solution(mesh):
    in_specs = (P("blk", None, "uly", None), P(), P(), P("uly", None), P("uly", None))
    out_specs = P("blk", None, "uly", None)
    return jax.shard_map(
        on_device, mesh=mesh, in_specs=in_specs, out_specs=out_specs, check_vma=False
    )
```

```python
import math

import jax
import jax.numpy as jnp
from jax import lax
from jax.sharding import PartitionSpec as P

HS = 64


def padded_2(shard, sides, width):
    for axis, dim in sides:
        size, length = (lax.axis_size(axis), shard.shape[dim])
        up = [(i, (i + 1) % size) for i in range(size - 1)]
        down = [(j, i) for i, j in up]
        last = lax.slice_in_dim(shard, length - width, length, axis=dim)
        initial = lax.slice_in_dim(shard, 0, width, axis=dim)
        before = lax.ppermute(last, axis, up)
        after = lax.ppermute(initial, axis, down)
        shard = jnp.concatenate([before, shard, after], axis=dim)
    return shard


def gathered(piece, axis):
    size = lax.axis_size(axis)
    parts = [piece]
    for shift in range(1, size):
        pairs = [(i, (i + shift) % size) for i in range(size)]
        parts.append(lax.ppermute(piece, axis, pairs))
    return jnp.concatenate(parts, axis=0)


def relayed(piece, axis):
    size = lax.axis_size(axis)
    half = size // 2
    if size % 2:
        return gathered(piece, axis)
    mirror = [(i, (i + half) % size) for i in range(size)]
    crossed = lax.ppermute(piece, axis, mirror)
    parts = [piece, crossed]
    for shift in range(1, half):
        pairs = [(i, (i // half) * half + (i % half + shift) % half) for i in range(size)]
        parts.append(lax.ppermute(piece, axis, pairs))
        parts.append(lax.ppermute(crossed, axis, pairs))
    return jnp.concatenate(parts, axis=0)


def chip_shift(size, shift):
    chips = size // 2
    return [(i, ((i // 2 + shift) % chips) * 2 + i % 2) for i in range(size)]


def gathered_by_chip(piece, axis):
    size = lax.axis_size(axis)
    rank = lax.axis_index(axis)
    chips, core = size // 2, rank % 2
    partner = [(i, i ^ 1) for i in range(size)]
    stacked = jnp.zeros((size,) + piece.shape, piece.dtype)
    stacked = lax.dynamic_update_index_in_dim(stacked, piece, rank, 0)
    near = lax.ppermute(piece, axis, partner)
    stacked = lax.dynamic_update_index_in_dim(stacked, near, rank ^ 1, 0)
    for shift in range(1, chips):
        source_chip = (rank // 2 - shift) % chips
        far = lax.ppermute(piece, axis, chip_shift(size, shift))
        stacked = lax.dynamic_update_index_in_dim(stacked, far, source_chip * 2 + core, 0)
        handed = lax.ppermute(far, axis, partner)
        stacked = lax.dynamic_update_index_in_dim(stacked, handed, source_chip * 2 + 1 - core, 0)
    return stacked


def scattered_sum_by_chip(whole, axis, shape):
    size = lax.axis_size(axis)
    rank = lax.axis_index(axis)
    chips, core, chip = size // 2, rank % 2, rank // 2
    blocks = whole.reshape(chips, 2, whole.shape[0] // size, *whole.shape[1:])
    mine = lax.dynamic_index_in_dim(blocks, core, 1, keepdims=False)
    theirs = lax.dynamic_index_in_dim(blocks, 1 - core, 1, keepdims=False)
    chip_sum = mine + lax.ppermute(theirs, axis, [(i, i ^ 1) for i in range(size)])
    total = lax.dynamic_index_in_dim(chip_sum, chip, 0, keepdims=False).reshape(shape)
    for shift in range(1, chips):
        outgoing = lax.dynamic_index_in_dim(chip_sum, (chip + shift) % chips, 0, keepdims=False)
        arrived = lax.ppermute(outgoing.astype(jnp.bfloat16), axis, chip_shift(size, shift))
        total = total + arrived.astype(jnp.float32).reshape(shape)
    return total


def scattered_sum(whole, axis):
    size = lax.axis_size(axis)
    rank = lax.axis_index(axis)
    blocks = whole.reshape(size, whole.shape[0] // size, *whole.shape[1:])
    total = lax.dynamic_index_in_dim(blocks, rank, 0, keepdims=False)
    for shift in range(1, size):
        pairs = [(i, (i + shift) % size) for i in range(size)]
        outgoing = lax.dynamic_index_in_dim(blocks, (rank + shift) % size, 0, keepdims=False)
        total = total + lax.ppermute(outgoing, axis, pairs)
    return total


def times_transposed(left, right):
    return lax.dot_general(
        left, right, (((1,), (1,)), ((), ())), preferred_element_type=jnp.float32
    )


def on_device(tokens, conv_weight, conv_bias, qkv_weight, out_weight):
    z_count, x_count, y_count, features = tokens.shape
    groups = lax.axis_size("uly")
    with_halo = padded_2(tokens, (("blk", 0),), 1)
    slab_in = gathered_by_chip(with_halo, "uly")
    slab_in = slab_in.transpose(1, 2, 0, 3, 4).reshape(
        z_count + 2, x_count, groups * y_count, features
    )
    slab_y = groups * y_count
    padded = jnp.pad(slab_in, ((0, 0), (1, 1), (1, 1), (0, 0)))
    summed = slab_in[1 : 1 + z_count].astype(jnp.float32) + conv_bias
    for step_z in range(3):
        for step_x in range(3):
            for step_y in range(3):
                summed = (
                    summed
                    + conv_weight[9 * step_z + 3 * step_x + step_y]
                    * padded[
                        step_z : step_z + z_count,
                        step_x : step_x + x_count,
                        step_y : step_y + slab_y,
                    ]
                )
    positioned = summed.astype(jnp.bfloat16)
    local_tok = z_count * x_count * y_count
    heads_here = qkv_weight.shape[0] // (3 * HS)
    slab_rows = (
        positioned.reshape(z_count, x_count, groups, y_count, features)
        .transpose(2, 0, 1, 3, 4)
        .reshape(groups * local_tok, features)
    )
    slab_tok = slab_rows.shape[0]
    head_weight = qkv_weight.reshape(heads_here, 3, HS, features)
    kv_weight = head_weight[:, 1:].reshape(heads_here * 2 * HS, features)
    q_weight = head_weight[:, 0].reshape(heads_here * HS, features)
    kv_rows = times_transposed(slab_rows, kv_weight).astype(jnp.bfloat16)
    key_value = relayed(kv_rows.reshape(slab_tok, heads_here, 2, HS), "blk")
    queries = times_transposed(slab_rows, q_weight).astype(jnp.bfloat16)
    queries = queries.reshape(slab_tok, heads_here, HS)
    key_piece = key_value[:, :, 0]
    value_piece = key_value[:, :, 1]
    score_scale = 1.0 / math.sqrt(HS)
    key_count = key_piece.shape[0]
    block_len = min(1024, key_count)
    key_blocks = key_piece.reshape(key_count // block_len, block_len, heads_here, HS)
    value_blocks = value_piece.reshape(key_count // block_len, block_len, heads_here, HS)

    def attend(query_rows):
        rows = query_rows.shape[0]

        def key_block(carry_state, key_value):
            running_max, running_sum, weighted = carry_state
            key_part, value_part = key_value
            scores = (
                jnp.einsum(
                    "qhd,khd->hqk", query_rows, key_part, preferred_element_type=jnp.float32
                )
                * score_scale
            )
            new_max = jnp.maximum(running_max, jnp.max(scores, axis=2))
            shrink = jnp.exp(running_max - new_max)
            weights = jnp.exp(scores - new_max[:, :, None])
            running_sum = running_sum * shrink + jnp.sum(weights, axis=2)
            weighted = weighted * shrink[:, :, None] + jnp.einsum(
                "hqk,khd->hqd",
                weights.astype(jnp.bfloat16),
                value_part,
                preferred_element_type=jnp.float32,
            )
            return ((new_max, running_sum, weighted), None)

        start_state = (
            jnp.full((heads_here, rows), -1e30, jnp.float32),
            jnp.zeros((heads_here, rows), jnp.float32),
            jnp.zeros((heads_here, rows, HS), jnp.float32),
        )
        folded, unused = lax.scan(key_block, start_state, (key_blocks, value_blocks))
        running_max, running_sum, weighted = folded
        attended = (weighted / running_sum[:, :, None]).astype(jnp.bfloat16)
        return attended.transpose(1, 0, 2).reshape(rows, heads_here * HS)

    rank = lax.axis_index("uly")
    chips, core, chip = groups // 2, rank % 2, rank // 2
    pair_queries = queries.reshape(chips, 2 * local_tok, heads_here, HS)
    total = None
    for shift in range(1, chips):
        far_rows = lax.dynamic_index_in_dim(pair_queries, (chip + shift) % chips, 0, keepdims=False)
        far_partial = jnp.dot(attend(far_rows), out_weight, preferred_element_type=jnp.float32)
        far_partial = far_partial.astype(jnp.bfloat16).reshape(2, local_tok, features)
        same_core = lax.dynamic_index_in_dim(far_partial, core, 0, keepdims=False)
        other_core = lax.dynamic_index_in_dim(far_partial, 1 - core, 0, keepdims=False)
        far_sent = (same_core, other_core)
        to_other_core = [
            (i, ((i // 2 + shift) % chips) * 2 + 1 - i % 2) for i in range(groups)
        ]
        for arrived in (
            lax.ppermute(same_core, "uly", chip_shift(groups, shift)),
            lax.ppermute(other_core, "uly", to_other_core),
        ):
            arrived = arrived.astype(jnp.float32).reshape(tokens.shape)
            total = arrived if total is None else total + arrived
    near_rows = lax.dynamic_index_in_dim(pair_queries, chip, 0, keepdims=False)
    if total is not None:
        near_rows, unused = lax.optimization_barrier((near_rows, far_sent))
    near_partial = jnp.dot(attend(near_rows), out_weight, preferred_element_type=jnp.float32)
    near_partial = near_partial.reshape(2, local_tok, features)
    own = lax.dynamic_index_in_dim(near_partial, core, 0, keepdims=False)
    for_partner = lax.dynamic_index_in_dim(near_partial, 1 - core, 0, keepdims=False)
    from_partner = lax.ppermute(for_partner, "uly", [(i, i ^ 1) for i in range(groups)])
    near_sum = own.reshape(tokens.shape) + from_partner.reshape(tokens.shape)
    result = near_sum if total is None else near_sum + total
    return result.astype(jnp.bfloat16)


def solution(mesh):
    in_specs = (P("blk", None, "uly", None), P(), P(), P("uly", None), P("uly", None))
    out_specs = P("blk", None, "uly", None)
    return jax.shard_map(
        on_device, mesh=mesh, in_specs=in_specs, out_specs=out_specs, check_vma=False
    )
```

```python
import math

import jax
import jax.numpy as jnp
from jax import lax
from jax.sharding import PartitionSpec as P

HS = 64


def padded_2(shard, sides, width):
    for axis, dim in sides:
        size, length = (lax.axis_size(axis), shard.shape[dim])
        up = [(i, (i + 1) % size) for i in range(size - 1)]
        down = [(j, i) for i, j in up]
        last = lax.slice_in_dim(shard, length - width, length, axis=dim)
        initial = lax.slice_in_dim(shard, 0, width, axis=dim)
        before = lax.ppermute(last, axis, up)
        after = lax.ppermute(initial, axis, down)
        shard = jnp.concatenate([before, shard, after], axis=dim)
    return shard


def gathered(piece, axis):
    size = lax.axis_size(axis)
    parts = [piece]
    for shift in range(1, size):
        pairs = [(i, (i + shift) % size) for i in range(size)]
        parts.append(lax.ppermute(piece, axis, pairs))
    return jnp.concatenate(parts, axis=0)


def relayed(piece, axis):
    size = lax.axis_size(axis)
    half = size // 2
    if size % 2:
        return gathered(piece, axis)
    mirror = [(i, (i + half) % size) for i in range(size)]
    crossed = lax.ppermute(piece, axis, mirror)
    parts = [piece, crossed]
    for shift in range(1, half):
        pairs = [(i, (i // half) * half + (i % half + shift) % half) for i in range(size)]
        parts.append(lax.ppermute(piece, axis, pairs))
        parts.append(lax.ppermute(crossed, axis, pairs))
    return jnp.concatenate(parts, axis=0)


def chip_shift(size, shift):
    chips = size // 2
    return [(i, ((i // 2 + shift) % chips) * 2 + i % 2) for i in range(size)]


def gathered_by_chip(piece, axis):
    size = lax.axis_size(axis)
    rank = lax.axis_index(axis)
    chips, core = size // 2, rank % 2
    partner = [(i, i ^ 1) for i in range(size)]
    stacked = jnp.zeros((size,) + piece.shape, piece.dtype)
    stacked = lax.dynamic_update_index_in_dim(stacked, piece, rank, 0)
    near = lax.ppermute(piece, axis, partner)
    stacked = lax.dynamic_update_index_in_dim(stacked, near, rank ^ 1, 0)
    for shift in range(1, chips):
        source_chip = (rank // 2 - shift) % chips
        far = lax.ppermute(piece, axis, chip_shift(size, shift))
        stacked = lax.dynamic_update_index_in_dim(stacked, far, source_chip * 2 + core, 0)
        handed = lax.ppermute(far, axis, partner)
        stacked = lax.dynamic_update_index_in_dim(stacked, handed, source_chip * 2 + 1 - core, 0)
    return stacked


def scattered_sum_by_chip(whole, axis, shape):
    size = lax.axis_size(axis)
    rank = lax.axis_index(axis)
    chips, core, chip = size // 2, rank % 2, rank // 2
    blocks = whole.reshape(chips, 2, whole.shape[0] // size, *whole.shape[1:])
    mine = lax.dynamic_index_in_dim(blocks, core, 1, keepdims=False)
    theirs = lax.dynamic_index_in_dim(blocks, 1 - core, 1, keepdims=False)
    chip_sum = mine + lax.ppermute(theirs, axis, [(i, i ^ 1) for i in range(size)])
    total = lax.dynamic_index_in_dim(chip_sum, chip, 0, keepdims=False).reshape(shape)
    for shift in range(1, chips):
        outgoing = lax.dynamic_index_in_dim(chip_sum, (chip + shift) % chips, 0, keepdims=False)
        arrived = lax.ppermute(outgoing.astype(jnp.bfloat16), axis, chip_shift(size, shift))
        total = total + arrived.astype(jnp.float32).reshape(shape)
    return total


def scattered_sum(whole, axis):
    size = lax.axis_size(axis)
    rank = lax.axis_index(axis)
    blocks = whole.reshape(size, whole.shape[0] // size, *whole.shape[1:])
    total = lax.dynamic_index_in_dim(blocks, rank, 0, keepdims=False)
    for shift in range(1, size):
        pairs = [(i, (i + shift) % size) for i in range(size)]
        outgoing = lax.dynamic_index_in_dim(blocks, (rank + shift) % size, 0, keepdims=False)
        total = total + lax.ppermute(outgoing, axis, pairs)
    return total


def times_transposed(left, right):
    return lax.dot_general(
        left, right, (((1,), (1,)), ((), ())), preferred_element_type=jnp.float32
    )


def on_device(tokens, conv_weight, conv_bias, qkv_weight, out_weight):
    z_count, x_count, y_count, features = tokens.shape
    groups = lax.axis_size("uly")
    with_halo = padded_2(tokens, (("blk", 0),), 1)
    slab_in = gathered_by_chip(with_halo, "uly")
    slab_in = slab_in.transpose(1, 2, 0, 3, 4).reshape(
        z_count + 2, x_count, groups * y_count, features
    )
    slab_y = groups * y_count
    padded = jnp.pad(slab_in, ((0, 0), (1, 1), (1, 1), (0, 0)))
    summed = slab_in[1 : 1 + z_count].astype(jnp.float32) + conv_bias
    for step_z in range(3):
        for step_x in range(3):
            for step_y in range(3):
                summed = (
                    summed
                    + conv_weight[9 * step_z + 3 * step_x + step_y]
                    * padded[
                        step_z : step_z + z_count,
                        step_x : step_x + x_count,
                        step_y : step_y + slab_y,
                    ]
                )
    positioned = summed.astype(jnp.bfloat16)
    local_tok = z_count * x_count * y_count
    heads_here = qkv_weight.shape[0] // (3 * HS)
    slab_rows = (
        positioned.reshape(z_count, x_count, groups, y_count, features)
        .transpose(2, 0, 1, 3, 4)
        .reshape(groups * local_tok, features)
    )
    slab_tok = slab_rows.shape[0]
    projected = times_transposed(slab_rows, qkv_weight).astype(jnp.bfloat16)
    split_heads = projected.reshape(slab_tok, heads_here, 3, HS)
    queries = split_heads[:, :, 0]
    key_value = relayed(split_heads[:, :, 1:], "blk")
    key_piece = key_value[:, :, 0]
    value_piece = key_value[:, :, 1]
    score_scale = 1.0 / math.sqrt(HS)
    key_count = key_piece.shape[0]
    block_len = min(1024, key_count)
    key_blocks = key_piece.reshape(key_count // block_len, block_len, heads_here, HS)
    value_blocks = value_piece.reshape(key_count // block_len, block_len, heads_here, HS)

    def attend(query_rows):
        rows = query_rows.shape[0]

        def key_block(carry_state, key_value):
            running_max, running_sum, weighted = carry_state
            key_part, value_part = key_value
            scores = (
                jnp.einsum(
                    "qhd,khd->hqk", query_rows, key_part, preferred_element_type=jnp.float32
                )
                * score_scale
            )
            new_max = jnp.maximum(running_max, jnp.max(scores, axis=2))
            shrink = jnp.exp(running_max - new_max)
            weights = jnp.exp(scores - new_max[:, :, None])
            running_sum = running_sum * shrink + jnp.sum(weights, axis=2)
            weighted = weighted * shrink[:, :, None] + jnp.einsum(
                "hqk,khd->hqd",
                weights.astype(jnp.bfloat16),
                value_part,
                preferred_element_type=jnp.float32,
            )
            return ((new_max, running_sum, weighted), None)

        start_state = (
            jnp.full((heads_here, rows), -1e30, jnp.float32),
            jnp.zeros((heads_here, rows), jnp.float32),
            jnp.zeros((heads_here, rows, HS), jnp.float32),
        )
        folded, unused = lax.scan(key_block, start_state, (key_blocks, value_blocks))
        running_max, running_sum, weighted = folded
        attended = (weighted / running_sum[:, :, None]).astype(jnp.bfloat16)
        return attended.transpose(1, 0, 2).reshape(rows, heads_here * HS)

    rank = lax.axis_index("uly")
    chips, core, chip = groups // 2, rank % 2, rank // 2
    pair_queries = queries.reshape(chips, 2 * local_tok, heads_here, HS)
    total = None
    partner = [(i, i ^ 1) for i in range(groups)]
    for shift in range(1, chips):
        far_rows = lax.dynamic_index_in_dim(pair_queries, (chip + shift) % chips, 0, keepdims=False)
        far_partial = jnp.dot(attend(far_rows), out_weight, preferred_element_type=jnp.float32)
        far_partial = far_partial.reshape(2, local_tok, features)
        mine = lax.dynamic_index_in_dim(far_partial, core, 0, keepdims=False)
        for_partner = lax.dynamic_index_in_dim(far_partial, 1 - core, 0, keepdims=False)
        far_sent = for_partner
        chip_sum = mine + lax.ppermute(for_partner, "uly", partner)
        arrived = lax.ppermute(chip_sum.astype(jnp.bfloat16), "uly", chip_shift(groups, shift))
        arrived = arrived.astype(jnp.float32).reshape(tokens.shape)
        total = arrived if total is None else total + arrived
    near_rows = lax.dynamic_index_in_dim(pair_queries, chip, 0, keepdims=False)
    if total is not None:
        near_rows, unused = lax.optimization_barrier((near_rows, far_sent))
    near_partial = jnp.dot(attend(near_rows), out_weight, preferred_element_type=jnp.float32)
    near_partial = near_partial.reshape(2, local_tok, features)
    own = lax.dynamic_index_in_dim(near_partial, core, 0, keepdims=False)
    for_partner = lax.dynamic_index_in_dim(near_partial, 1 - core, 0, keepdims=False)
    from_partner = lax.ppermute(for_partner, "uly", partner)
    near_sum = own.reshape(tokens.shape) + from_partner.reshape(tokens.shape)
    result = near_sum if total is None else near_sum + total
    return result.astype(jnp.bfloat16)


def solution(mesh):
    in_specs = (P("blk", None, "uly", None), P(), P(), P("uly", None), P("uly", None))
    out_specs = P("blk", None, "uly", None)
    return jax.shard_map(
        on_device, mesh=mesh, in_specs=in_specs, out_specs=out_specs, check_vma=False
    )
```

```python
import math

import jax
import jax.numpy as jnp
from jax import lax
from jax.sharding import PartitionSpec as P

HS = 64


def padded_2(shard, sides, width):
    for axis, dim in sides:
        size, length = (lax.axis_size(axis), shard.shape[dim])
        up = [(i, (i + 1) % size) for i in range(size - 1)]
        down = [(j, i) for i, j in up]
        last = lax.slice_in_dim(shard, length - width, length, axis=dim)
        initial = lax.slice_in_dim(shard, 0, width, axis=dim)
        before = lax.ppermute(last, axis, up)
        after = lax.ppermute(initial, axis, down)
        shard = jnp.concatenate([before, shard, after], axis=dim)
    return shard


def gathered(piece, axis):
    size = lax.axis_size(axis)
    parts = [piece]
    for shift in range(1, size):
        pairs = [(i, (i + shift) % size) for i in range(size)]
        parts.append(lax.ppermute(piece, axis, pairs))
    return jnp.concatenate(parts, axis=0)


def relayed(piece, axis):
    size = lax.axis_size(axis)
    half = size // 2
    if size % 2:
        return gathered(piece, axis)
    mirror = [(i, (i + half) % size) for i in range(size)]
    crossed = lax.ppermute(piece, axis, mirror)
    parts = [piece, crossed]
    for shift in range(1, half):
        pairs = [(i, (i // half) * half + (i % half + shift) % half) for i in range(size)]
        parts.append(lax.ppermute(piece, axis, pairs))
        parts.append(lax.ppermute(crossed, axis, pairs))
    return jnp.concatenate(parts, axis=0)


def chip_shift(size, shift):
    chips = size // 2
    return [(i, ((i // 2 + shift) % chips) * 2 + i % 2) for i in range(size)]


def gathered_by_chip(piece, axis):
    size = lax.axis_size(axis)
    rank = lax.axis_index(axis)
    chips, core = size // 2, rank % 2
    partner = [(i, i ^ 1) for i in range(size)]
    stacked = jnp.zeros((size,) + piece.shape, piece.dtype)
    stacked = lax.dynamic_update_index_in_dim(stacked, piece, rank, 0)
    near = lax.ppermute(piece, axis, partner)
    stacked = lax.dynamic_update_index_in_dim(stacked, near, rank ^ 1, 0)
    halves = 2 if piece.ndim > 1 and piece.shape[1] % 2 == 0 else 1
    width = piece.shape[1] // halves
    zeros = (0,) * (piece.ndim - 1)
    for shift in range(1, chips):
        source_chip = (rank // 2 - shift) % chips
        for half in range(halves):
            part = lax.slice_in_dim(piece, half * width, (half + 1) * width, axis=1)
            far = lax.ppermute(part, axis, chip_shift(size, shift))
            start = (source_chip * 2 + core, 0, half * width) + zeros[1:]
            stacked = lax.dynamic_update_slice(stacked, far[None], start)
            handed = lax.ppermute(far, axis, partner)
            start = (source_chip * 2 + 1 - core, 0, half * width) + zeros[1:]
            stacked = lax.dynamic_update_slice(stacked, handed[None], start)
    return stacked


def scattered_sum_by_chip(whole, axis, shape):
    size = lax.axis_size(axis)
    rank = lax.axis_index(axis)
    chips, core, chip = size // 2, rank % 2, rank // 2
    blocks = whole.reshape(chips, 2, whole.shape[0] // size, *whole.shape[1:])
    mine = lax.dynamic_index_in_dim(blocks, core, 1, keepdims=False)
    theirs = lax.dynamic_index_in_dim(blocks, 1 - core, 1, keepdims=False)
    chip_sum = mine + lax.ppermute(theirs, axis, [(i, i ^ 1) for i in range(size)])
    total = lax.dynamic_index_in_dim(chip_sum, chip, 0, keepdims=False).reshape(shape)
    for shift in range(1, chips):
        outgoing = lax.dynamic_index_in_dim(chip_sum, (chip + shift) % chips, 0, keepdims=False)
        arrived = lax.ppermute(outgoing.astype(jnp.bfloat16), axis, chip_shift(size, shift))
        total = total + arrived.astype(jnp.float32).reshape(shape)
    return total


def scattered_sum(whole, axis):
    size = lax.axis_size(axis)
    rank = lax.axis_index(axis)
    blocks = whole.reshape(size, whole.shape[0] // size, *whole.shape[1:])
    total = lax.dynamic_index_in_dim(blocks, rank, 0, keepdims=False)
    for shift in range(1, size):
        pairs = [(i, (i + shift) % size) for i in range(size)]
        outgoing = lax.dynamic_index_in_dim(blocks, (rank + shift) % size, 0, keepdims=False)
        total = total + lax.ppermute(outgoing, axis, pairs)
    return total


def times_transposed(left, right):
    return lax.dot_general(
        left, right, (((1,), (1,)), ((), ())), preferred_element_type=jnp.float32
    )


def on_device(tokens, conv_weight, conv_bias, qkv_weight, out_weight):
    z_count, x_count, y_count, features = tokens.shape
    groups = lax.axis_size("uly")
    with_halo = padded_2(tokens, (("blk", 0),), 1)
    slab_in = gathered_by_chip(with_halo, "uly")
    slab_in = slab_in.transpose(1, 2, 0, 3, 4).reshape(
        z_count + 2, x_count, groups * y_count, features
    )
    slab_y = groups * y_count
    padded = jnp.pad(slab_in, ((0, 0), (1, 1), (1, 1), (0, 0)))
    summed = slab_in[1 : 1 + z_count].astype(jnp.float32) + conv_bias
    for step_z in range(3):
        for step_x in range(3):
            for step_y in range(3):
                summed = (
                    summed
                    + conv_weight[9 * step_z + 3 * step_x + step_y]
                    * padded[
                        step_z : step_z + z_count,
                        step_x : step_x + x_count,
                        step_y : step_y + slab_y,
                    ]
                )
    positioned = summed.astype(jnp.bfloat16)
    local_tok = z_count * x_count * y_count
    heads_here = qkv_weight.shape[0] // (3 * HS)
    slab_rows = (
        positioned.reshape(z_count, x_count, groups, y_count, features)
        .transpose(2, 0, 1, 3, 4)
        .reshape(groups * local_tok, features)
    )
    slab_tok = slab_rows.shape[0]
    projected = times_transposed(slab_rows, qkv_weight).astype(jnp.bfloat16)
    split_heads = projected.reshape(slab_tok, heads_here, 3, HS)
    queries = split_heads[:, :, 0]
    key_value = relayed(split_heads[:, :, 1:], "blk")
    key_piece = key_value[:, :, 0]
    value_piece = key_value[:, :, 1]
    score_scale = 1.0 / math.sqrt(HS)
    key_count = key_piece.shape[0]
    block_len = min(1024, key_count)
    key_blocks = key_piece.reshape(key_count // block_len, block_len, heads_here, HS)
    value_blocks = value_piece.reshape(key_count // block_len, block_len, heads_here, HS)

    def attend(query_rows):
        rows = query_rows.shape[0]

        def key_block(carry_state, key_value):
            running_max, running_sum, weighted = carry_state
            key_part, value_part = key_value
            scores = (
                jnp.einsum(
                    "qhd,khd->hqk", query_rows, key_part, preferred_element_type=jnp.float32
                )
                * score_scale
            )
            new_max = jnp.maximum(running_max, jnp.max(scores, axis=2))
            shrink = jnp.exp(running_max - new_max)
            weights = jnp.exp(scores - new_max[:, :, None])
            running_sum = running_sum * shrink + jnp.sum(weights, axis=2)
            weighted = weighted * shrink[:, :, None] + jnp.einsum(
                "hqk,khd->hqd",
                weights.astype(jnp.bfloat16),
                value_part,
                preferred_element_type=jnp.float32,
            )
            return ((new_max, running_sum, weighted), None)

        start_state = (
            jnp.full((heads_here, rows), -1e30, jnp.float32),
            jnp.zeros((heads_here, rows), jnp.float32),
            jnp.zeros((heads_here, rows, HS), jnp.float32),
        )
        folded, unused = lax.scan(key_block, start_state, (key_blocks, value_blocks))
        running_max, running_sum, weighted = folded
        attended = (weighted / running_sum[:, :, None]).astype(jnp.bfloat16)
        return attended.transpose(1, 0, 2).reshape(rows, heads_here * HS)

    rank = lax.axis_index("uly")
    chips, core, chip = groups // 2, rank % 2, rank // 2
    pair_queries = queries.reshape(chips, 2 * local_tok, heads_here, HS)
    total = None
    for shift in range(1, chips):
        far_rows = lax.dynamic_index_in_dim(pair_queries, (chip + shift) % chips, 0, keepdims=False)
        far_partial = jnp.dot(attend(far_rows), out_weight, preferred_element_type=jnp.float32)
        far_partial = far_partial.astype(jnp.bfloat16).reshape(2, local_tok, features)
        same_core = lax.dynamic_index_in_dim(far_partial, core, 0, keepdims=False)
        other_core = lax.dynamic_index_in_dim(far_partial, 1 - core, 0, keepdims=False)
        far_sent = (same_core, other_core)
        to_other_core = [
            (i, ((i // 2 + shift) % chips) * 2 + 1 - i % 2) for i in range(groups)
        ]
        for arrived in (
            lax.ppermute(same_core, "uly", chip_shift(groups, shift)),
            lax.ppermute(other_core, "uly", to_other_core),
        ):
            arrived = arrived.astype(jnp.float32).reshape(tokens.shape)
            total = arrived if total is None else total + arrived
    near_rows = lax.dynamic_index_in_dim(pair_queries, chip, 0, keepdims=False)
    if total is not None:
        near_rows, unused = lax.optimization_barrier((near_rows, far_sent))
    near_partial = jnp.dot(attend(near_rows), out_weight, preferred_element_type=jnp.float32)
    near_partial = near_partial.reshape(2, local_tok, features)
    own = lax.dynamic_index_in_dim(near_partial, core, 0, keepdims=False)
    for_partner = lax.dynamic_index_in_dim(near_partial, 1 - core, 0, keepdims=False)
    from_partner = lax.ppermute(for_partner, "uly", [(i, i ^ 1) for i in range(groups)])
    near_sum = own.reshape(tokens.shape) + from_partner.reshape(tokens.shape)
    result = near_sum if total is None else near_sum + total
    return result.astype(jnp.bfloat16)


def solution(mesh):
    in_specs = (P("blk", None, "uly", None), P(), P(), P("uly", None), P("uly", None))
    out_specs = P("blk", None, "uly", None)
    return jax.shard_map(
        on_device, mesh=mesh, in_specs=in_specs, out_specs=out_specs, check_vma=False
    )
```

```python
import math

import jax
import jax.numpy as jnp
from jax import lax
from jax.sharding import PartitionSpec as P

HS = 64


def padded_2(shard, sides, width):
    for axis, dim in sides:
        size, length = (lax.axis_size(axis), shard.shape[dim])
        up = [(i, (i + 1) % size) for i in range(size - 1)]
        down = [(j, i) for i, j in up]
        last = lax.slice_in_dim(shard, length - width, length, axis=dim)
        initial = lax.slice_in_dim(shard, 0, width, axis=dim)
        before = lax.ppermute(last, axis, up)
        after = lax.ppermute(initial, axis, down)
        shard = jnp.concatenate([before, shard, after], axis=dim)
    return shard


def gathered(piece, axis):
    size = lax.axis_size(axis)
    parts = [piece]
    for shift in range(1, size):
        pairs = [(i, (i + shift) % size) for i in range(size)]
        parts.append(lax.ppermute(piece, axis, pairs))
    return jnp.concatenate(parts, axis=0)


def relayed(piece, axis):
    size = lax.axis_size(axis)
    half = size // 2
    if size % 2:
        return gathered(piece, axis)
    mirror = [(i, (i + half) % size) for i in range(size)]
    crossed = lax.ppermute(piece, axis, mirror)
    parts = [piece, crossed]
    for shift in range(1, half):
        pairs = [(i, (i // half) * half + (i % half + shift) % half) for i in range(size)]
        parts.append(lax.ppermute(piece, axis, pairs))
        parts.append(lax.ppermute(crossed, axis, pairs))
    return jnp.concatenate(parts, axis=0)


def chip_shift(size, shift):
    chips = size // 2
    return [(i, ((i // 2 + shift) % chips) * 2 + i % 2) for i in range(size)]


def gathered_by_chip(piece, axis):
    size = lax.axis_size(axis)
    rank = lax.axis_index(axis)
    chips, core = size // 2, rank % 2
    partner = [(i, i ^ 1) for i in range(size)]
    stacked = jnp.zeros((size,) + piece.shape, piece.dtype)
    stacked = lax.dynamic_update_index_in_dim(stacked, piece, rank, 0)
    near = lax.ppermute(piece, axis, partner)
    stacked = lax.dynamic_update_index_in_dim(stacked, near, rank ^ 1, 0)
    for shift in range(1, chips):
        source_chip = (rank // 2 - shift) % chips
        far = lax.ppermute(piece, axis, chip_shift(size, shift))
        stacked = lax.dynamic_update_index_in_dim(stacked, far, source_chip * 2 + core, 0)
        handed = lax.ppermute(far, axis, partner)
        stacked = lax.dynamic_update_index_in_dim(stacked, handed, source_chip * 2 + 1 - core, 0)
    return stacked


def scattered_sum_by_chip(whole, axis, shape):
    size = lax.axis_size(axis)
    rank = lax.axis_index(axis)
    chips, core, chip = size // 2, rank % 2, rank // 2
    blocks = whole.reshape(chips, 2, whole.shape[0] // size, *whole.shape[1:])
    mine = lax.dynamic_index_in_dim(blocks, core, 1, keepdims=False)
    theirs = lax.dynamic_index_in_dim(blocks, 1 - core, 1, keepdims=False)
    chip_sum = mine + lax.ppermute(theirs, axis, [(i, i ^ 1) for i in range(size)])
    total = lax.dynamic_index_in_dim(chip_sum, chip, 0, keepdims=False).reshape(shape)
    for shift in range(1, chips):
        outgoing = lax.dynamic_index_in_dim(chip_sum, (chip + shift) % chips, 0, keepdims=False)
        arrived = lax.ppermute(outgoing.astype(jnp.bfloat16), axis, chip_shift(size, shift))
        total = total + arrived.astype(jnp.float32).reshape(shape)
    return total


def scattered_sum(whole, axis):
    size = lax.axis_size(axis)
    rank = lax.axis_index(axis)
    blocks = whole.reshape(size, whole.shape[0] // size, *whole.shape[1:])
    total = lax.dynamic_index_in_dim(blocks, rank, 0, keepdims=False)
    for shift in range(1, size):
        pairs = [(i, (i + shift) % size) for i in range(size)]
        outgoing = lax.dynamic_index_in_dim(blocks, (rank + shift) % size, 0, keepdims=False)
        total = total + lax.ppermute(outgoing, axis, pairs)
    return total


def times_transposed(left, right):
    return lax.dot_general(
        left, right, (((1,), (1,)), ((), ())), preferred_element_type=jnp.float32
    )


def on_device(tokens, conv_weight, conv_bias, qkv_weight, out_weight):
    z_count, x_count, y_count, features = tokens.shape
    groups = lax.axis_size("uly")
    with_halo = padded_2(tokens, (("blk", 0),), 1)
    slab_in = lax.all_gather(with_halo, "uly", axis=0, tiled=False)
    slab_in = slab_in.transpose(1, 2, 0, 3, 4).reshape(
        z_count + 2, x_count, groups * y_count, features
    )
    slab_y = groups * y_count
    padded = jnp.pad(slab_in, ((0, 0), (1, 1), (1, 1), (0, 0)))
    summed = slab_in[1 : 1 + z_count].astype(jnp.float32) + conv_bias
    for step_z in range(3):
        for step_x in range(3):
            for step_y in range(3):
                summed = (
                    summed
                    + conv_weight[9 * step_z + 3 * step_x + step_y]
                    * padded[
                        step_z : step_z + z_count,
                        step_x : step_x + x_count,
                        step_y : step_y + slab_y,
                    ]
                )
    positioned = summed.astype(jnp.bfloat16)
    local_tok = z_count * x_count * y_count
    heads_here = qkv_weight.shape[0] // (3 * HS)
    slab_rows = (
        positioned.reshape(z_count, x_count, groups, y_count, features)
        .transpose(2, 0, 1, 3, 4)
        .reshape(groups * local_tok, features)
    )
    slab_tok = slab_rows.shape[0]
    projected = times_transposed(slab_rows, qkv_weight).astype(jnp.bfloat16)
    split_heads = projected.reshape(slab_tok, heads_here, 3, HS)
    queries = split_heads[:, :, 0]
    key_value = relayed(split_heads[:, :, 1:], "blk")
    key_piece = key_value[:, :, 0]
    value_piece = key_value[:, :, 1]
    score_scale = 1.0 / math.sqrt(HS)
    key_count = key_piece.shape[0]
    block_len = min(1024, key_count)
    key_blocks = key_piece.reshape(key_count // block_len, block_len, heads_here, HS)
    value_blocks = value_piece.reshape(key_count // block_len, block_len, heads_here, HS)

    def attend(query_rows):
        rows = query_rows.shape[0]

        def key_block(carry_state, key_value):
            running_max, running_sum, weighted = carry_state
            key_part, value_part = key_value
            scores = (
                jnp.einsum(
                    "qhd,khd->hqk", query_rows, key_part, preferred_element_type=jnp.float32
                )
                * score_scale
            )
            new_max = jnp.maximum(running_max, jnp.max(scores, axis=2))
            shrink = jnp.exp(running_max - new_max)
            weights = jnp.exp(scores - new_max[:, :, None])
            running_sum = running_sum * shrink + jnp.sum(weights, axis=2)
            weighted = weighted * shrink[:, :, None] + jnp.einsum(
                "hqk,khd->hqd",
                weights.astype(jnp.bfloat16),
                value_part,
                preferred_element_type=jnp.float32,
            )
            return ((new_max, running_sum, weighted), None)

        start_state = (
            jnp.full((heads_here, rows), -1e30, jnp.float32),
            jnp.zeros((heads_here, rows), jnp.float32),
            jnp.zeros((heads_here, rows, HS), jnp.float32),
        )
        folded, unused = lax.scan(key_block, start_state, (key_blocks, value_blocks))
        running_max, running_sum, weighted = folded
        attended = (weighted / running_sum[:, :, None]).astype(jnp.bfloat16)
        return attended.transpose(1, 0, 2).reshape(rows, heads_here * HS)

    rank = lax.axis_index("uly")
    chips, core, chip = groups // 2, rank % 2, rank // 2
    pair_queries = queries.reshape(chips, 2 * local_tok, heads_here, HS)
    total = None
    for shift in range(1, chips):
        far_rows = lax.dynamic_index_in_dim(pair_queries, (chip + shift) % chips, 0, keepdims=False)
        far_partial = jnp.dot(attend(far_rows), out_weight, preferred_element_type=jnp.float32)
        far_partial = far_partial.astype(jnp.bfloat16).reshape(2, local_tok, features)
        same_core = lax.dynamic_index_in_dim(far_partial, core, 0, keepdims=False)
        other_core = lax.dynamic_index_in_dim(far_partial, 1 - core, 0, keepdims=False)
        far_sent = (same_core, other_core)
        to_other_core = [
            (i, ((i // 2 + shift) % chips) * 2 + 1 - i % 2) for i in range(groups)
        ]
        for arrived in (
            lax.ppermute(same_core, "uly", chip_shift(groups, shift)),
            lax.ppermute(other_core, "uly", to_other_core),
        ):
            arrived = arrived.astype(jnp.float32).reshape(tokens.shape)
            total = arrived if total is None else total + arrived
    near_rows = lax.dynamic_index_in_dim(pair_queries, chip, 0, keepdims=False)
    if total is not None:
        near_rows, unused = lax.optimization_barrier((near_rows, far_sent))
    near_partial = jnp.dot(attend(near_rows), out_weight, preferred_element_type=jnp.float32)
    near_partial = near_partial.reshape(2, local_tok, features)
    own = lax.dynamic_index_in_dim(near_partial, core, 0, keepdims=False)
    for_partner = lax.dynamic_index_in_dim(near_partial, 1 - core, 0, keepdims=False)
    from_partner = lax.ppermute(for_partner, "uly", [(i, i ^ 1) for i in range(groups)])
    near_sum = own.reshape(tokens.shape) + from_partner.reshape(tokens.shape)
    result = near_sum if total is None else near_sum + total
    return result.astype(jnp.bfloat16)


def solution(mesh):
    in_specs = (P("blk", None, "uly", None), P(), P(), P("uly", None), P("uly", None))
    out_specs = P("blk", None, "uly", None)
    return jax.shard_map(
        on_device, mesh=mesh, in_specs=in_specs, out_specs=out_specs, check_vma=False
    )
```

```python
import math

import jax
import jax.numpy as jnp
from jax import lax
from jax.sharding import PartitionSpec as P

HS = 64


def padded_2(shard, sides, width):
    for axis, dim in sides:
        size, length = (lax.axis_size(axis), shard.shape[dim])
        up = [(i, (i + 1) % size) for i in range(size - 1)]
        down = [(j, i) for i, j in up]
        last = lax.slice_in_dim(shard, length - width, length, axis=dim)
        initial = lax.slice_in_dim(shard, 0, width, axis=dim)
        before = lax.ppermute(last, axis, up)
        after = lax.ppermute(initial, axis, down)
        shard = jnp.concatenate([before, shard, after], axis=dim)
    return shard


def gathered(piece, axis):
    size = lax.axis_size(axis)
    parts = [piece]
    for shift in range(1, size):
        pairs = [(i, (i + shift) % size) for i in range(size)]
        parts.append(lax.ppermute(piece, axis, pairs))
    return jnp.concatenate(parts, axis=0)


def relayed(piece, axis):
    size = lax.axis_size(axis)
    half = size // 2
    if size % 2:
        return gathered(piece, axis)
    mirror = [(i, (i + half) % size) for i in range(size)]
    crossed = lax.ppermute(piece, axis, mirror)
    parts = [piece, crossed]
    for shift in range(1, half):
        pairs = [(i, (i // half) * half + (i % half + shift) % half) for i in range(size)]
        parts.append(lax.ppermute(piece, axis, pairs))
        parts.append(lax.ppermute(crossed, axis, pairs))
    return jnp.concatenate(parts, axis=0)


def chip_shift(size, shift):
    chips = size // 2
    return [(i, ((i // 2 + shift) % chips) * 2 + i % 2) for i in range(size)]


def gathered_by_chip(piece, axis):
    size = lax.axis_size(axis)
    rank = lax.axis_index(axis)
    chips, core = size // 2, rank % 2
    partner = [(i, i ^ 1) for i in range(size)]
    stacked = jnp.zeros((size,) + piece.shape, piece.dtype)
    stacked = lax.dynamic_update_index_in_dim(stacked, piece, rank, 0)
    near = lax.ppermute(piece, axis, partner)
    stacked = lax.dynamic_update_index_in_dim(stacked, near, rank ^ 1, 0)
    for shift in range(1, chips):
        source_chip = (rank // 2 - shift) % chips
        far = lax.ppermute(piece, axis, chip_shift(size, shift))
        stacked = lax.dynamic_update_index_in_dim(stacked, far, source_chip * 2 + core, 0)
        handed = lax.ppermute(far, axis, partner)
        stacked = lax.dynamic_update_index_in_dim(stacked, handed, source_chip * 2 + 1 - core, 0)
    return stacked


def scattered_sum_by_chip(whole, axis, shape):
    size = lax.axis_size(axis)
    rank = lax.axis_index(axis)
    chips, core, chip = size // 2, rank % 2, rank // 2
    blocks = whole.reshape(chips, 2, whole.shape[0] // size, *whole.shape[1:])
    mine = lax.dynamic_index_in_dim(blocks, core, 1, keepdims=False)
    theirs = lax.dynamic_index_in_dim(blocks, 1 - core, 1, keepdims=False)
    chip_sum = mine + lax.ppermute(theirs, axis, [(i, i ^ 1) for i in range(size)])
    total = lax.dynamic_index_in_dim(chip_sum, chip, 0, keepdims=False).reshape(shape)
    for shift in range(1, chips):
        outgoing = lax.dynamic_index_in_dim(chip_sum, (chip + shift) % chips, 0, keepdims=False)
        arrived = lax.ppermute(outgoing.astype(jnp.bfloat16), axis, chip_shift(size, shift))
        total = total + arrived.astype(jnp.float32).reshape(shape)
    return total


def scattered_sum(whole, axis):
    size = lax.axis_size(axis)
    rank = lax.axis_index(axis)
    blocks = whole.reshape(size, whole.shape[0] // size, *whole.shape[1:])
    total = lax.dynamic_index_in_dim(blocks, rank, 0, keepdims=False)
    for shift in range(1, size):
        pairs = [(i, (i + shift) % size) for i in range(size)]
        outgoing = lax.dynamic_index_in_dim(blocks, (rank + shift) % size, 0, keepdims=False)
        total = total + lax.ppermute(outgoing, axis, pairs)
    return total


def times_transposed(left, right):
    return lax.dot_general(
        left, right, (((1,), (1,)), ((), ())), preferred_element_type=jnp.float32
    )


def on_device(tokens, conv_weight, conv_bias, qkv_weight, out_weight):
    z_count, x_count, y_count, features = tokens.shape
    groups = lax.axis_size("uly")
    with_halo = padded_2(tokens, (("blk", 0),), 1)
    slab_in = gathered_by_chip(with_halo, "uly")
    slab_in = slab_in.transpose(1, 2, 0, 3, 4).reshape(
        z_count + 2, x_count, groups * y_count, features
    )
    slab_y = groups * y_count
    padded = jnp.pad(slab_in, ((0, 0), (1, 1), (1, 1), (0, 0)))
    summed = slab_in[1 : 1 + z_count].astype(jnp.float32) + conv_bias
    for step_z in range(3):
        for step_x in range(3):
            for step_y in range(3):
                summed = (
                    summed
                    + conv_weight[9 * step_z + 3 * step_x + step_y]
                    * padded[
                        step_z : step_z + z_count,
                        step_x : step_x + x_count,
                        step_y : step_y + slab_y,
                    ]
                )
    positioned = summed.astype(jnp.bfloat16)
    local_tok = z_count * x_count * y_count
    heads_here = qkv_weight.shape[0] // (3 * HS)
    slab_rows = (
        positioned.reshape(z_count, x_count, groups, y_count, features)
        .transpose(2, 0, 1, 3, 4)
        .reshape(groups * local_tok, features)
    )
    slab_tok = slab_rows.shape[0]
    projected = times_transposed(slab_rows, qkv_weight).astype(jnp.bfloat16)
    split_heads = projected.reshape(slab_tok, heads_here, 3, HS)
    queries = split_heads[:, :, 0]
    key_value = relayed(split_heads[:, :, 1:], "blk")
    key_piece = key_value[:, :, 0]
    value_piece = key_value[:, :, 1]
    score_scale = 1.0 / math.sqrt(HS)
    key_count = key_piece.shape[0]
    block_len = min(1024, key_count)
    key_blocks = key_piece.reshape(key_count // block_len, block_len, heads_here, HS)
    value_blocks = value_piece.reshape(key_count // block_len, block_len, heads_here, HS)

    def attend(query_rows):
        rows = query_rows.shape[0]

        def key_block(carry_state, key_value):
            running_max, running_sum, weighted = carry_state
            key_part, value_part = key_value
            scores = (
                jnp.einsum(
                    "qhd,khd->hqk", query_rows, key_part, preferred_element_type=jnp.float32
                )
                * score_scale
            )
            new_max = jnp.maximum(running_max, jnp.max(scores, axis=2))
            shrink = jnp.exp(running_max - new_max)
            weights = jnp.exp(scores - new_max[:, :, None])
            running_sum = running_sum * shrink + jnp.sum(weights, axis=2)
            weighted = weighted * shrink[:, :, None] + jnp.einsum(
                "hqk,khd->hqd",
                weights.astype(jnp.bfloat16),
                value_part,
                preferred_element_type=jnp.float32,
            )
            return ((new_max, running_sum, weighted), None)

        if key_blocks.shape[0] == 1:
            scores = (
                jnp.einsum(
                    "qhd,khd->hqk", query_rows, key_piece, preferred_element_type=jnp.float32
                )
                * score_scale
            )
            row_max = jnp.max(scores, axis=2, keepdims=True)
            weights = jnp.exp(scores - row_max)
            row_sum = jnp.sum(weights, axis=2, keepdims=True)
            mixed = jnp.einsum(
                "hqk,khd->hqd",
                weights.astype(jnp.bfloat16),
                value_piece,
                preferred_element_type=jnp.float32,
            )
            attended = (mixed / row_sum).astype(jnp.bfloat16)
            return attended.transpose(1, 0, 2).reshape(rows, heads_here * HS)

        start_state = (
            jnp.full((heads_here, rows), -1e30, jnp.float32),
            jnp.zeros((heads_here, rows), jnp.float32),
            jnp.zeros((heads_here, rows, HS), jnp.float32),
        )
        folded, unused = lax.scan(key_block, start_state, (key_blocks, value_blocks))
        running_max, running_sum, weighted = folded
        attended = (weighted / running_sum[:, :, None]).astype(jnp.bfloat16)
        return attended.transpose(1, 0, 2).reshape(rows, heads_here * HS)

    rank = lax.axis_index("uly")
    chips, core, chip = groups // 2, rank % 2, rank // 2
    pair_queries = queries.reshape(chips, 2 * local_tok, heads_here, HS)
    total = None
    for shift in range(1, chips):
        far_rows = lax.dynamic_index_in_dim(pair_queries, (chip + shift) % chips, 0, keepdims=False)
        far_partial = jnp.dot(attend(far_rows), out_weight, preferred_element_type=jnp.float32)
        far_partial = far_partial.astype(jnp.bfloat16).reshape(2, local_tok, features)
        same_core = lax.dynamic_index_in_dim(far_partial, core, 0, keepdims=False)
        other_core = lax.dynamic_index_in_dim(far_partial, 1 - core, 0, keepdims=False)
        far_sent = (same_core, other_core)
        to_other_core = [
            (i, ((i // 2 + shift) % chips) * 2 + 1 - i % 2) for i in range(groups)
        ]
        for arrived in (
            lax.ppermute(same_core, "uly", chip_shift(groups, shift)),
            lax.ppermute(other_core, "uly", to_other_core),
        ):
            arrived = arrived.astype(jnp.float32).reshape(tokens.shape)
            total = arrived if total is None else total + arrived
    near_rows = lax.dynamic_index_in_dim(pair_queries, chip, 0, keepdims=False)
    if total is not None:
        near_rows, unused = lax.optimization_barrier((near_rows, far_sent))
    near_partial = jnp.dot(attend(near_rows), out_weight, preferred_element_type=jnp.float32)
    near_partial = near_partial.reshape(2, local_tok, features)
    own = lax.dynamic_index_in_dim(near_partial, core, 0, keepdims=False)
    for_partner = lax.dynamic_index_in_dim(near_partial, 1 - core, 0, keepdims=False)
    from_partner = lax.ppermute(for_partner, "uly", [(i, i ^ 1) for i in range(groups)])
    near_sum = own.reshape(tokens.shape) + from_partner.reshape(tokens.shape)
    result = near_sum if total is None else near_sum + total
    return result.astype(jnp.bfloat16)


def solution(mesh):
    in_specs = (P("blk", None, "uly", None), P(), P(), P("uly", None), P("uly", None))
    out_specs = P("blk", None, "uly", None)
    return jax.shard_map(
        on_device, mesh=mesh, in_specs=in_specs, out_specs=out_specs, check_vma=False
    )
```

```python
import math

import jax
import jax.numpy as jnp
from jax import lax
from jax.experimental.layout import Layout, with_layout_constraint
from jax.sharding import PartitionSpec as P

HS = 64


def padded_2(shard, sides, width, keep=None):
    for axis, dim in sides:
        size, length = (lax.axis_size(axis), shard.shape[dim])
        up = [(i, (i + 1) % size) for i in range(size - 1)]
        down = [(j, i) for i, j in up]
        last = lax.slice_in_dim(shard, length - width, length, axis=dim)
        initial = lax.slice_in_dim(shard, 0, width, axis=dim)
        if keep is not None:
            last = with_layout_constraint(last, keep)
            initial = with_layout_constraint(initial, keep)
        before = lax.ppermute(last, axis, up)
        after = lax.ppermute(initial, axis, down)
        shard = jnp.concatenate([before, shard, after], axis=dim)
    return shard


def gathered(piece, axis):
    size = lax.axis_size(axis)
    parts = [piece]
    for shift in range(1, size):
        pairs = [(i, (i + shift) % size) for i in range(size)]
        parts.append(lax.ppermute(piece, axis, pairs))
    return jnp.concatenate(parts, axis=0)


def relayed(piece, axis):
    size = lax.axis_size(axis)
    half = size // 2
    if size % 2:
        return gathered(piece, axis)
    mirror = [(i, (i + half) % size) for i in range(size)]
    crossed = lax.ppermute(piece, axis, mirror)
    parts = [piece, crossed]
    for shift in range(1, half):
        pairs = [(i, (i // half) * half + (i % half + shift) % half) for i in range(size)]
        parts.append(lax.ppermute(piece, axis, pairs))
        parts.append(lax.ppermute(crossed, axis, pairs))
    return jnp.concatenate(parts, axis=0)


def chip_shift(size, shift):
    chips = size // 2
    return [(i, ((i // 2 + shift) % chips) * 2 + i % 2) for i in range(size)]


def gathered_by_chip(piece, axis):
    size = lax.axis_size(axis)
    rank = lax.axis_index(axis)
    chips, core = size // 2, rank % 2
    partner = [(i, i ^ 1) for i in range(size)]
    stacked = jnp.zeros((size,) + piece.shape, piece.dtype)
    stacked = lax.dynamic_update_index_in_dim(stacked, piece, rank, 0)
    near = lax.ppermute(piece, axis, partner)
    stacked = lax.dynamic_update_index_in_dim(stacked, near, rank ^ 1, 0)
    for shift in range(1, chips):
        source_chip = (rank // 2 - shift) % chips
        far = lax.ppermute(piece, axis, chip_shift(size, shift))
        stacked = lax.dynamic_update_index_in_dim(stacked, far, source_chip * 2 + core, 0)
        handed = lax.ppermute(far, axis, partner)
        stacked = lax.dynamic_update_index_in_dim(stacked, handed, source_chip * 2 + 1 - core, 0)
    return stacked


def scattered_sum_by_chip(whole, axis, shape):
    size = lax.axis_size(axis)
    rank = lax.axis_index(axis)
    chips, core, chip = size // 2, rank % 2, rank // 2
    blocks = whole.reshape(chips, 2, whole.shape[0] // size, *whole.shape[1:])
    mine = lax.dynamic_index_in_dim(blocks, core, 1, keepdims=False)
    theirs = lax.dynamic_index_in_dim(blocks, 1 - core, 1, keepdims=False)
    chip_sum = mine + lax.ppermute(theirs, axis, [(i, i ^ 1) for i in range(size)])
    total = lax.dynamic_index_in_dim(chip_sum, chip, 0, keepdims=False).reshape(shape)
    for shift in range(1, chips):
        outgoing = lax.dynamic_index_in_dim(chip_sum, (chip + shift) % chips, 0, keepdims=False)
        arrived = lax.ppermute(outgoing.astype(jnp.bfloat16), axis, chip_shift(size, shift))
        total = total + arrived.astype(jnp.float32).reshape(shape)
    return total


def scattered_sum(whole, axis):
    size = lax.axis_size(axis)
    rank = lax.axis_index(axis)
    blocks = whole.reshape(size, whole.shape[0] // size, *whole.shape[1:])
    total = lax.dynamic_index_in_dim(blocks, rank, 0, keepdims=False)
    for shift in range(1, size):
        pairs = [(i, (i + shift) % size) for i in range(size)]
        outgoing = lax.dynamic_index_in_dim(blocks, (rank + shift) % size, 0, keepdims=False)
        total = total + lax.ppermute(outgoing, axis, pairs)
    return total


def times_transposed(left, right):
    return lax.dot_general(
        left, right, (((1,), (1,)), ((), ())), preferred_element_type=jnp.float32
    )


def on_device(tokens, conv_weight, conv_bias, qkv_weight, out_weight):
    z_count, x_count, y_count, features = tokens.shape
    groups = lax.axis_size("uly")
    arrival = Layout(major_to_minor=tuple(range(tokens.ndim)))
    with_halo = padded_2(tokens, (("blk", 0),), 1, arrival if y_count == 2 else None)
    slab_in = gathered_by_chip(with_halo, "uly")
    slab_in = slab_in.transpose(1, 2, 0, 3, 4).reshape(
        z_count + 2, x_count, groups * y_count, features
    )
    slab_y = groups * y_count
    padded = jnp.pad(slab_in, ((0, 0), (1, 1), (1, 1), (0, 0)))
    summed = slab_in[1 : 1 + z_count].astype(jnp.float32) + conv_bias
    for step_z in range(3):
        for step_x in range(3):
            for step_y in range(3):
                summed = (
                    summed
                    + conv_weight[9 * step_z + 3 * step_x + step_y]
                    * padded[
                        step_z : step_z + z_count,
                        step_x : step_x + x_count,
                        step_y : step_y + slab_y,
                    ]
                )
    positioned = summed.astype(jnp.bfloat16)
    local_tok = z_count * x_count * y_count
    heads_here = qkv_weight.shape[0] // (3 * HS)
    slab_rows = (
        positioned.reshape(z_count, x_count, groups, y_count, features)
        .transpose(2, 0, 1, 3, 4)
        .reshape(groups * local_tok, features)
    )
    slab_tok = slab_rows.shape[0]
    projected = times_transposed(slab_rows, qkv_weight).astype(jnp.bfloat16)
    split_heads = projected.reshape(slab_tok, heads_here, 3, HS)
    queries = split_heads[:, :, 0]
    key_value = relayed(split_heads[:, :, 1:], "blk")
    key_piece = key_value[:, :, 0]
    value_piece = key_value[:, :, 1]
    score_scale = 1.0 / math.sqrt(HS)
    key_count = key_piece.shape[0]
    block_len = min(1024, key_count)
    key_blocks = key_piece.reshape(key_count // block_len, block_len, heads_here, HS)
    value_blocks = value_piece.reshape(key_count // block_len, block_len, heads_here, HS)

    def attend(query_rows):
        rows = query_rows.shape[0]

        def key_block(carry_state, key_value):
            running_max, running_sum, weighted = carry_state
            key_part, value_part = key_value
            scores = (
                jnp.einsum(
                    "qhd,khd->hqk", query_rows, key_part, preferred_element_type=jnp.float32
                )
                * score_scale
            )
            new_max = jnp.maximum(running_max, jnp.max(scores, axis=2))
            shrink = jnp.exp(running_max - new_max)
            weights = jnp.exp(scores - new_max[:, :, None])
            running_sum = running_sum * shrink + jnp.sum(weights, axis=2)
            weighted = weighted * shrink[:, :, None] + jnp.einsum(
                "hqk,khd->hqd",
                weights.astype(jnp.bfloat16),
                value_part,
                preferred_element_type=jnp.float32,
            )
            return ((new_max, running_sum, weighted), None)

        start_state = (
            jnp.full((heads_here, rows), -1e30, jnp.float32),
            jnp.zeros((heads_here, rows), jnp.float32),
            jnp.zeros((heads_here, rows, HS), jnp.float32),
        )
        folded, unused = lax.scan(key_block, start_state, (key_blocks, value_blocks))
        running_max, running_sum, weighted = folded
        attended = (weighted / running_sum[:, :, None]).astype(jnp.bfloat16)
        return attended.transpose(1, 0, 2).reshape(rows, heads_here * HS)

    rank = lax.axis_index("uly")
    chips, core, chip = groups // 2, rank % 2, rank // 2
    pair_queries = queries.reshape(chips, 2 * local_tok, heads_here, HS)
    total = None
    for shift in range(1, chips):
        far_rows = lax.dynamic_index_in_dim(pair_queries, (chip + shift) % chips, 0, keepdims=False)
        far_partial = jnp.dot(attend(far_rows), out_weight, preferred_element_type=jnp.float32)
        far_partial = far_partial.astype(jnp.bfloat16).reshape(2, local_tok, features)
        same_core = lax.dynamic_index_in_dim(far_partial, core, 0, keepdims=False)
        other_core = lax.dynamic_index_in_dim(far_partial, 1 - core, 0, keepdims=False)
        far_sent = (same_core, other_core)
        to_other_core = [
            (i, ((i // 2 + shift) % chips) * 2 + 1 - i % 2) for i in range(groups)
        ]
        for arrived in (
            lax.ppermute(same_core, "uly", chip_shift(groups, shift)),
            lax.ppermute(other_core, "uly", to_other_core),
        ):
            arrived = arrived.astype(jnp.float32).reshape(tokens.shape)
            total = arrived if total is None else total + arrived
    near_rows = lax.dynamic_index_in_dim(pair_queries, chip, 0, keepdims=False)
    if total is not None:
        near_rows, unused = lax.optimization_barrier((near_rows, far_sent))
    near_partial = jnp.dot(attend(near_rows), out_weight, preferred_element_type=jnp.float32)
    near_partial = near_partial.reshape(2, local_tok, features)
    own = lax.dynamic_index_in_dim(near_partial, core, 0, keepdims=False)
    for_partner = lax.dynamic_index_in_dim(near_partial, 1 - core, 0, keepdims=False)
    from_partner = lax.ppermute(for_partner, "uly", [(i, i ^ 1) for i in range(groups)])
    near_sum = own.reshape(tokens.shape) + from_partner.reshape(tokens.shape)
    result = near_sum if total is None else near_sum + total
    return result.astype(jnp.bfloat16)


def solution(mesh):
    in_specs = (P("blk", None, "uly", None), P(), P(), P("uly", None), P("uly", None))
    out_specs = P("blk", None, "uly", None)
    return jax.shard_map(
        on_device, mesh=mesh, in_specs=in_specs, out_specs=out_specs, check_vma=False
    )
```

```python
import math

import jax
import jax.numpy as jnp
from jax import lax
from jax.experimental.layout import Layout, with_layout_constraint
from jax.sharding import PartitionSpec as P

HS = 64


def padded_2(shard, sides, width, keep=None):
    for axis, dim in sides:
        size, length = (lax.axis_size(axis), shard.shape[dim])
        up = [(i, (i + 1) % size) for i in range(size - 1)]
        down = [(j, i) for i, j in up]
        last = lax.slice_in_dim(shard, length - width, length, axis=dim)
        initial = lax.slice_in_dim(shard, 0, width, axis=dim)
        if keep is not None:
            last = with_layout_constraint(last, keep)
            initial = with_layout_constraint(initial, keep)
        before = lax.ppermute(last, axis, up)
        after = lax.ppermute(initial, axis, down)
        shard = jnp.concatenate([before, shard, after], axis=dim)
    return shard


def gathered(piece, axis):
    size = lax.axis_size(axis)
    parts = [piece]
    for shift in range(1, size):
        pairs = [(i, (i + shift) % size) for i in range(size)]
        parts.append(lax.ppermute(piece, axis, pairs))
    return jnp.concatenate(parts, axis=0)


def relayed(piece, axis):
    size = lax.axis_size(axis)
    half = size // 2
    if size % 2:
        return gathered(piece, axis)
    mirror = [(i, (i + half) % size) for i in range(size)]
    crossed = lax.ppermute(piece, axis, mirror)
    parts = [piece, crossed]
    for shift in range(1, half):
        pairs = [(i, (i // half) * half + (i % half + shift) % half) for i in range(size)]
        parts.append(lax.ppermute(piece, axis, pairs))
        parts.append(lax.ppermute(crossed, axis, pairs))
    return jnp.concatenate(parts, axis=0)


def chip_shift(size, shift):
    chips = size // 2
    return [(i, ((i // 2 + shift) % chips) * 2 + i % 2) for i in range(size)]


def gathered_by_chip(piece, axis):
    size = lax.axis_size(axis)
    rank = lax.axis_index(axis)
    chips, core = size // 2, rank % 2
    partner = [(i, i ^ 1) for i in range(size)]
    stacked = jnp.zeros((size,) + piece.shape, piece.dtype)
    stacked = lax.dynamic_update_index_in_dim(stacked, piece, rank, 0)
    near = lax.ppermute(piece, axis, partner)
    stacked = lax.dynamic_update_index_in_dim(stacked, near, rank ^ 1, 0)
    for shift in range(1, chips):
        source_chip = (rank // 2 - shift) % chips
        far = lax.ppermute(piece, axis, chip_shift(size, shift))
        stacked = lax.dynamic_update_index_in_dim(stacked, far, source_chip * 2 + core, 0)
        handed = lax.ppermute(far, axis, partner)
        stacked = lax.dynamic_update_index_in_dim(stacked, handed, source_chip * 2 + 1 - core, 0)
    return stacked


def scattered_sum_by_chip(whole, axis, shape):
    size = lax.axis_size(axis)
    rank = lax.axis_index(axis)
    chips, core, chip = size // 2, rank % 2, rank // 2
    blocks = whole.reshape(chips, 2, whole.shape[0] // size, *whole.shape[1:])
    mine = lax.dynamic_index_in_dim(blocks, core, 1, keepdims=False)
    theirs = lax.dynamic_index_in_dim(blocks, 1 - core, 1, keepdims=False)
    chip_sum = mine + lax.ppermute(theirs, axis, [(i, i ^ 1) for i in range(size)])
    total = lax.dynamic_index_in_dim(chip_sum, chip, 0, keepdims=False).reshape(shape)
    for shift in range(1, chips):
        outgoing = lax.dynamic_index_in_dim(chip_sum, (chip + shift) % chips, 0, keepdims=False)
        arrived = lax.ppermute(outgoing.astype(jnp.bfloat16), axis, chip_shift(size, shift))
        total = total + arrived.astype(jnp.float32).reshape(shape)
    return total


def scattered_sum(whole, axis):
    size = lax.axis_size(axis)
    rank = lax.axis_index(axis)
    blocks = whole.reshape(size, whole.shape[0] // size, *whole.shape[1:])
    total = lax.dynamic_index_in_dim(blocks, rank, 0, keepdims=False)
    for shift in range(1, size):
        pairs = [(i, (i + shift) % size) for i in range(size)]
        outgoing = lax.dynamic_index_in_dim(blocks, (rank + shift) % size, 0, keepdims=False)
        total = total + lax.ppermute(outgoing, axis, pairs)
    return total


def times_transposed(left, right):
    return lax.dot_general(
        left, right, (((1,), (1,)), ((), ())), preferred_element_type=jnp.float32
    )


def on_device(tokens, conv_weight, conv_bias, qkv_weight, out_weight):
    z_count, x_count, y_count, features = tokens.shape
    groups = lax.axis_size("uly")
    arrival = Layout(major_to_minor=tuple(range(tokens.ndim)))
    with_halo = padded_2(tokens, (("blk", 0),), 1, arrival if y_count == 2 else None)
    slab_in = gathered_by_chip(with_halo, "uly")
    slab_in = slab_in.transpose(1, 2, 0, 3, 4).reshape(
        z_count + 2, x_count, groups * y_count, features
    )
    slab_y = groups * y_count
    padded = jnp.pad(slab_in, ((0, 0), (1, 1), (1, 1), (0, 0)))
    summed = slab_in[1 : 1 + z_count].astype(jnp.float32) + conv_bias
    for step_z in range(3):
        for step_x in range(3):
            for step_y in range(3):
                summed = (
                    summed
                    + conv_weight[9 * step_z + 3 * step_x + step_y]
                    * padded[
                        step_z : step_z + z_count,
                        step_x : step_x + x_count,
                        step_y : step_y + slab_y,
                    ]
                )
    positioned = summed.astype(jnp.bfloat16)
    local_tok = z_count * x_count * y_count
    heads_here = qkv_weight.shape[0] // (3 * HS)
    slab_rows = (
        positioned.reshape(z_count, x_count, groups, y_count, features)
        .transpose(2, 0, 1, 3, 4)
        .reshape(groups * local_tok, features)
    )
    slab_tok = slab_rows.shape[0]
    projected = times_transposed(slab_rows, qkv_weight).astype(jnp.bfloat16)
    split_heads = projected.reshape(slab_tok, heads_here, 3, HS)
    queries = split_heads[:, :, 0]
    key_value = relayed(split_heads[:, :, 1:], "blk")
    key_piece = key_value[:, :, 0]
    value_piece = key_value[:, :, 1]
    score_scale = 1.0 / math.sqrt(HS)
    key_count = key_piece.shape[0]
    block_len = min(1024, key_count)
    key_blocks = key_piece.reshape(key_count // block_len, block_len, heads_here, HS)
    value_blocks = value_piece.reshape(key_count // block_len, block_len, heads_here, HS)

    def attend(query_rows):
        rows = query_rows.shape[0]

        def key_block(carry_state, key_value):
            running_max, running_sum, weighted = carry_state
            key_part, value_part = key_value
            scores = (
                jnp.einsum(
                    "qhd,khd->hqk", query_rows, key_part, preferred_element_type=jnp.float32
                )
                * score_scale
            )
            new_max = jnp.maximum(running_max, jnp.max(scores, axis=2))
            shrink = jnp.exp(running_max - new_max)
            weights = jnp.exp(scores - new_max[:, :, None])
            running_sum = running_sum * shrink + jnp.sum(weights, axis=2)
            weighted = weighted * shrink[:, :, None] + jnp.einsum(
                "hqk,khd->hqd",
                weights.astype(jnp.bfloat16),
                value_part,
                preferred_element_type=jnp.float32,
            )
            return ((new_max, running_sum, weighted), None)

        start_state = (
            jnp.full((heads_here, rows), -1e30, jnp.float32),
            jnp.zeros((heads_here, rows), jnp.float32),
            jnp.zeros((heads_here, rows, HS), jnp.float32),
        )
        folded, unused = lax.scan(key_block, start_state, (key_blocks, value_blocks))
        running_max, running_sum, weighted = folded
        attended = (weighted / running_sum[:, :, None]).astype(jnp.bfloat16)
        return attended.transpose(1, 0, 2).reshape(rows, heads_here * HS)

    rank = lax.axis_index("uly")
    chips, core, chip = groups // 2, rank % 2, rank // 2
    pair_queries = queries.reshape(chips, 2 * local_tok, heads_here, HS)
    total = None
    for shift in range(1, chips):
        far_rows = lax.dynamic_index_in_dim(pair_queries, (chip + shift) % chips, 0, keepdims=False)
        far_partial = jnp.dot(attend(far_rows), out_weight, preferred_element_type=jnp.float32)
        far_partial = far_partial.astype(jnp.bfloat16).reshape(2, local_tok, features)
        same_core = lax.dynamic_index_in_dim(far_partial, core, 0, keepdims=False)
        other_core = lax.dynamic_index_in_dim(far_partial, 1 - core, 0, keepdims=False)
        far_sent = (same_core, other_core)
        to_other_core = [
            (i, ((i // 2 + shift) % chips) * 2 + 1 - i % 2) for i in range(groups)
        ]
        for arrived in (
            lax.ppermute(same_core, "uly", chip_shift(groups, shift)),
            lax.ppermute(other_core, "uly", to_other_core),
        ):
            arrived = arrived.astype(jnp.float32).reshape(tokens.shape)
            total = arrived if total is None else total + arrived
    near_rows = lax.dynamic_index_in_dim(pair_queries, chip, 0, keepdims=False)
    if total is not None:
        near_rows, unused = lax.optimization_barrier((near_rows, far_sent))
    near_partial = jnp.dot(attend(near_rows), out_weight, preferred_element_type=jnp.float32)
    near_partial = near_partial.reshape(2, local_tok, features)
    own = lax.dynamic_index_in_dim(near_partial, core, 0, keepdims=False)
    for_partner = lax.dynamic_index_in_dim(near_partial, 1 - core, 0, keepdims=False)
    from_partner = lax.ppermute(for_partner, "uly", [(i, i ^ 1) for i in range(groups)])
    near_sum = own.reshape(tokens.shape) + from_partner.reshape(tokens.shape)
    near_sum = with_layout_constraint(near_sum, Layout(major_to_minor=tuple(range(tokens.ndim))))
    result = near_sum if total is None else near_sum + total
    return result.astype(jnp.bfloat16)


def solution(mesh):
    in_specs = (P("blk", None, "uly", None), P(), P(), P("uly", None), P("uly", None))
    out_specs = P("blk", None, "uly", None)
    return jax.shard_map(
        on_device, mesh=mesh, in_specs=in_specs, out_specs=out_specs, check_vma=False
    )
```

```python
import math

import jax
import jax.numpy as jnp
from jax import lax
from jax.experimental.layout import Layout, with_layout_constraint
from jax.sharding import PartitionSpec as P

HS = 64


def padded_2(shard, sides, width, keep=None):
    for axis, dim in sides:
        size, length = (lax.axis_size(axis), shard.shape[dim])
        up = [(i, (i + 1) % size) for i in range(size - 1)]
        down = [(j, i) for i, j in up]
        last = lax.slice_in_dim(shard, length - width, length, axis=dim)
        initial = lax.slice_in_dim(shard, 0, width, axis=dim)
        if keep is not None:
            last = with_layout_constraint(last, keep)
            initial = with_layout_constraint(initial, keep)
        before = lax.ppermute(last, axis, up)
        after = lax.ppermute(initial, axis, down)
        shard = jnp.concatenate([before, shard, after], axis=dim)
    return shard


def gathered(piece, axis):
    size = lax.axis_size(axis)
    parts = [piece]
    for shift in range(1, size):
        pairs = [(i, (i + shift) % size) for i in range(size)]
        parts.append(lax.ppermute(piece, axis, pairs))
    return jnp.concatenate(parts, axis=0)


def relayed(piece, axis):
    size = lax.axis_size(axis)
    half = size // 2
    if size % 2:
        return gathered(piece, axis)
    mirror = [(i, (i + half) % size) for i in range(size)]
    crossed = lax.ppermute(piece, axis, mirror)
    parts = [piece, crossed]
    for shift in range(1, half):
        pairs = [(i, (i // half) * half + (i % half + shift) % half) for i in range(size)]
        parts.append(lax.ppermute(piece, axis, pairs))
        parts.append(lax.ppermute(crossed, axis, pairs))
    return jnp.concatenate(parts, axis=0)


def chip_shift(size, shift):
    chips = size // 2
    return [(i, ((i // 2 + shift) % chips) * 2 + i % 2) for i in range(size)]


def gathered_by_chip(piece, axis):
    size = lax.axis_size(axis)
    rank = lax.axis_index(axis)
    chips, core = size // 2, rank % 2
    partner = [(i, i ^ 1) for i in range(size)]
    stacked = jnp.zeros((size,) + piece.shape, piece.dtype)
    stacked = lax.dynamic_update_index_in_dim(stacked, piece, rank, 0)
    near = lax.ppermute(piece, axis, partner)
    stacked = lax.dynamic_update_index_in_dim(stacked, near, rank ^ 1, 0)
    for shift in range(1, chips):
        source_chip = (rank // 2 - shift) % chips
        far = lax.ppermute(piece, axis, chip_shift(size, shift))
        stacked = lax.dynamic_update_index_in_dim(stacked, far, source_chip * 2 + core, 0)
        handed = lax.ppermute(far, axis, partner)
        stacked = lax.dynamic_update_index_in_dim(stacked, handed, source_chip * 2 + 1 - core, 0)
    return stacked


def scattered_sum_by_chip(whole, axis, shape):
    size = lax.axis_size(axis)
    rank = lax.axis_index(axis)
    chips, core, chip = size // 2, rank % 2, rank // 2
    blocks = whole.reshape(chips, 2, whole.shape[0] // size, *whole.shape[1:])
    mine = lax.dynamic_index_in_dim(blocks, core, 1, keepdims=False)
    theirs = lax.dynamic_index_in_dim(blocks, 1 - core, 1, keepdims=False)
    chip_sum = mine + lax.ppermute(theirs, axis, [(i, i ^ 1) for i in range(size)])
    total = lax.dynamic_index_in_dim(chip_sum, chip, 0, keepdims=False).reshape(shape)
    for shift in range(1, chips):
        outgoing = lax.dynamic_index_in_dim(chip_sum, (chip + shift) % chips, 0, keepdims=False)
        arrived = lax.ppermute(outgoing.astype(jnp.bfloat16), axis, chip_shift(size, shift))
        total = total + arrived.astype(jnp.float32).reshape(shape)
    return total


def scattered_sum(whole, axis):
    size = lax.axis_size(axis)
    rank = lax.axis_index(axis)
    blocks = whole.reshape(size, whole.shape[0] // size, *whole.shape[1:])
    total = lax.dynamic_index_in_dim(blocks, rank, 0, keepdims=False)
    for shift in range(1, size):
        pairs = [(i, (i + shift) % size) for i in range(size)]
        outgoing = lax.dynamic_index_in_dim(blocks, (rank + shift) % size, 0, keepdims=False)
        total = total + lax.ppermute(outgoing, axis, pairs)
    return total


def times_transposed(left, right):
    return lax.dot_general(
        left, right, (((1,), (1,)), ((), ())), preferred_element_type=jnp.float32
    )


def on_device(tokens, conv_weight, conv_bias, qkv_weight, out_weight):
    z_count, x_count, y_count, features = tokens.shape
    groups = lax.axis_size("uly")
    arrival = Layout(major_to_minor=tuple(range(tokens.ndim)))
    with_halo = padded_2(tokens, (("blk", 0),), 1, arrival if y_count == 2 else None)
    slab_in = gathered_by_chip(with_halo, "uly")
    slab_in = slab_in.transpose(1, 2, 0, 3, 4).reshape(
        z_count + 2, x_count, groups * y_count, features
    )
    slab_y = groups * y_count
    padded = jnp.pad(slab_in, ((0, 0), (1, 1), (1, 1), (0, 0)))
    summed = slab_in[1 : 1 + z_count].astype(jnp.float32) + conv_bias
    for step_z in range(3):
        for step_x in range(3):
            for step_y in range(3):
                summed = (
                    summed
                    + conv_weight[9 * step_z + 3 * step_x + step_y]
                    * padded[
                        step_z : step_z + z_count,
                        step_x : step_x + x_count,
                        step_y : step_y + slab_y,
                    ]
                )
    positioned = summed.astype(jnp.bfloat16)
    local_tok = z_count * x_count * y_count
    heads_here = qkv_weight.shape[0] // (3 * HS)
    slab_rows = (
        positioned.reshape(z_count, x_count, groups, y_count, features)
        .transpose(2, 0, 1, 3, 4)
        .reshape(groups * local_tok, features)
    )
    slab_tok = slab_rows.shape[0]
    projected = times_transposed(slab_rows, qkv_weight).astype(jnp.bfloat16)
    projected = with_layout_constraint(projected, Layout(major_to_minor=(1, 0)))
    split_heads = projected.reshape(slab_tok, heads_here, 3, HS)
    queries = split_heads[:, :, 0]
    key_value = relayed(split_heads[:, :, 1:], "blk")
    key_piece = key_value[:, :, 0]
    value_piece = key_value[:, :, 1]
    score_scale = 1.0 / math.sqrt(HS)
    key_count = key_piece.shape[0]
    block_len = min(1024, key_count)
    key_blocks = key_piece.reshape(key_count // block_len, block_len, heads_here, HS)
    value_blocks = value_piece.reshape(key_count // block_len, block_len, heads_here, HS)

    def attend(query_rows):
        rows = query_rows.shape[0]

        def key_block(carry_state, key_value):
            running_max, running_sum, weighted = carry_state
            key_part, value_part = key_value
            scores = (
                jnp.einsum(
                    "qhd,khd->hqk", query_rows, key_part, preferred_element_type=jnp.float32
                )
                * score_scale
            )
            new_max = jnp.maximum(running_max, jnp.max(scores, axis=2))
            shrink = jnp.exp(running_max - new_max)
            weights = jnp.exp(scores - new_max[:, :, None])
            running_sum = running_sum * shrink + jnp.sum(weights, axis=2)
            weighted = weighted * shrink[:, :, None] + jnp.einsum(
                "hqk,khd->hqd",
                weights.astype(jnp.bfloat16),
                value_part,
                preferred_element_type=jnp.float32,
            )
            return ((new_max, running_sum, weighted), None)

        start_state = (
            jnp.full((heads_here, rows), -1e30, jnp.float32),
            jnp.zeros((heads_here, rows), jnp.float32),
            jnp.zeros((heads_here, rows, HS), jnp.float32),
        )
        folded, unused = lax.scan(key_block, start_state, (key_blocks, value_blocks))
        running_max, running_sum, weighted = folded
        attended = (weighted / running_sum[:, :, None]).astype(jnp.bfloat16)
        return attended.transpose(1, 0, 2).reshape(rows, heads_here * HS)

    rank = lax.axis_index("uly")
    chips, core, chip = groups // 2, rank % 2, rank // 2
    pair_queries = queries.reshape(chips, 2 * local_tok, heads_here, HS)
    total = None
    for shift in range(1, chips):
        far_rows = lax.dynamic_index_in_dim(pair_queries, (chip + shift) % chips, 0, keepdims=False)
        far_partial = jnp.dot(attend(far_rows), out_weight, preferred_element_type=jnp.float32)
        far_partial = far_partial.astype(jnp.bfloat16).reshape(2, local_tok, features)
        same_core = lax.dynamic_index_in_dim(far_partial, core, 0, keepdims=False)
        other_core = lax.dynamic_index_in_dim(far_partial, 1 - core, 0, keepdims=False)
        far_sent = (same_core, other_core)
        to_other_core = [
            (i, ((i // 2 + shift) % chips) * 2 + 1 - i % 2) for i in range(groups)
        ]
        for arrived in (
            lax.ppermute(same_core, "uly", chip_shift(groups, shift)),
            lax.ppermute(other_core, "uly", to_other_core),
        ):
            arrived = arrived.astype(jnp.float32).reshape(tokens.shape)
            total = arrived if total is None else total + arrived
    near_rows = lax.dynamic_index_in_dim(pair_queries, chip, 0, keepdims=False)
    if total is not None:
        near_rows, unused = lax.optimization_barrier((near_rows, far_sent))
    near_partial = jnp.dot(attend(near_rows), out_weight, preferred_element_type=jnp.float32)
    near_partial = near_partial.reshape(2, local_tok, features)
    own = lax.dynamic_index_in_dim(near_partial, core, 0, keepdims=False)
    for_partner = lax.dynamic_index_in_dim(near_partial, 1 - core, 0, keepdims=False)
    from_partner = lax.ppermute(for_partner, "uly", [(i, i ^ 1) for i in range(groups)])
    near_sum = own.reshape(tokens.shape) + from_partner.reshape(tokens.shape)
    result = near_sum if total is None else near_sum + total
    return result.astype(jnp.bfloat16)


def solution(mesh):
    in_specs = (P("blk", None, "uly", None), P(), P(), P("uly", None), P("uly", None))
    out_specs = P("blk", None, "uly", None)
    return jax.shard_map(
        on_device, mesh=mesh, in_specs=in_specs, out_specs=out_specs, check_vma=False
    )
```

```python
import math

import jax
import jax.numpy as jnp
from jax import lax
from jax.experimental.layout import Layout, with_layout_constraint
from jax.sharding import PartitionSpec as P

HS = 64


def padded_2(shard, sides, width, keep=None):
    for axis, dim in sides:
        size, length = (lax.axis_size(axis), shard.shape[dim])
        up = [(i, (i + 1) % size) for i in range(size - 1)]
        down = [(j, i) for i, j in up]
        last = lax.slice_in_dim(shard, length - width, length, axis=dim)
        initial = lax.slice_in_dim(shard, 0, width, axis=dim)
        if keep is not None:
            last = with_layout_constraint(last, keep)
            initial = with_layout_constraint(initial, keep)
        before = lax.ppermute(last, axis, up)
        after = lax.ppermute(initial, axis, down)
        shard = jnp.concatenate([before, shard, after], axis=dim)
    return shard


def gathered(piece, axis):
    size = lax.axis_size(axis)
    parts = [piece]
    for shift in range(1, size):
        pairs = [(i, (i + shift) % size) for i in range(size)]
        parts.append(lax.ppermute(piece, axis, pairs))
    return jnp.concatenate(parts, axis=0)


def relayed(piece, axis):
    size = lax.axis_size(axis)
    half = size // 2
    if size % 2:
        return gathered(piece, axis)
    mirror = [(i, (i + half) % size) for i in range(size)]
    crossed = lax.ppermute(piece, axis, mirror)
    parts = [piece, crossed]
    for shift in range(1, half):
        pairs = [(i, (i // half) * half + (i % half + shift) % half) for i in range(size)]
        parts.append(lax.ppermute(piece, axis, pairs))
        parts.append(lax.ppermute(crossed, axis, pairs))
    return jnp.concatenate(parts, axis=0)


def chip_shift(size, shift):
    chips = size // 2
    return [(i, ((i // 2 + shift) % chips) * 2 + i % 2) for i in range(size)]


def gathered_by_chip(piece, axis):
    size = lax.axis_size(axis)
    rank = lax.axis_index(axis)
    chips, core = size // 2, rank % 2
    partner = [(i, i ^ 1) for i in range(size)]
    stacked = jnp.zeros((size,) + piece.shape, piece.dtype)
    stacked = lax.dynamic_update_index_in_dim(stacked, piece, rank, 0)
    near = lax.ppermute(piece, axis, partner)
    stacked = lax.dynamic_update_index_in_dim(stacked, near, rank ^ 1, 0)
    for shift in range(1, chips):
        source_chip = (rank // 2 - shift) % chips
        far = lax.ppermute(piece, axis, chip_shift(size, shift))
        stacked = lax.dynamic_update_index_in_dim(stacked, far, source_chip * 2 + core, 0)
        handed = lax.ppermute(far, axis, partner)
        stacked = lax.dynamic_update_index_in_dim(stacked, handed, source_chip * 2 + 1 - core, 0)
    return stacked


def scattered_sum_by_chip(whole, axis, shape):
    size = lax.axis_size(axis)
    rank = lax.axis_index(axis)
    chips, core, chip = size // 2, rank % 2, rank // 2
    blocks = whole.reshape(chips, 2, whole.shape[0] // size, *whole.shape[1:])
    mine = lax.dynamic_index_in_dim(blocks, core, 1, keepdims=False)
    theirs = lax.dynamic_index_in_dim(blocks, 1 - core, 1, keepdims=False)
    chip_sum = mine + lax.ppermute(theirs, axis, [(i, i ^ 1) for i in range(size)])
    total = lax.dynamic_index_in_dim(chip_sum, chip, 0, keepdims=False).reshape(shape)
    for shift in range(1, chips):
        outgoing = lax.dynamic_index_in_dim(chip_sum, (chip + shift) % chips, 0, keepdims=False)
        arrived = lax.ppermute(outgoing.astype(jnp.bfloat16), axis, chip_shift(size, shift))
        total = total + arrived.astype(jnp.float32).reshape(shape)
    return total


def scattered_sum(whole, axis):
    size = lax.axis_size(axis)
    rank = lax.axis_index(axis)
    blocks = whole.reshape(size, whole.shape[0] // size, *whole.shape[1:])
    total = lax.dynamic_index_in_dim(blocks, rank, 0, keepdims=False)
    for shift in range(1, size):
        pairs = [(i, (i + shift) % size) for i in range(size)]
        outgoing = lax.dynamic_index_in_dim(blocks, (rank + shift) % size, 0, keepdims=False)
        total = total + lax.ppermute(outgoing, axis, pairs)
    return total


def times_transposed(left, right):
    return lax.dot_general(
        left, right, (((1,), (1,)), ((), ())), preferred_element_type=jnp.float32
    )


def on_device(tokens, conv_weight, conv_bias, qkv_weight, out_weight):
    z_count, x_count, y_count, features = tokens.shape
    groups = lax.axis_size("uly")
    arrival = Layout(major_to_minor=tuple(range(tokens.ndim)))
    with_halo = padded_2(tokens, (("blk", 0),), 1, arrival if y_count == 2 else None)
    slab_in = gathered_by_chip(with_halo, "uly")
    slab_in = slab_in.transpose(1, 2, 0, 3, 4).reshape(
        z_count + 2, x_count, groups * y_count, features
    )
    slab_y = groups * y_count
    padded = jnp.pad(slab_in, ((0, 0), (1, 1), (1, 1), (0, 0)))
    summed = slab_in[1 : 1 + z_count].astype(jnp.float32) + conv_bias
    for step_z in range(3):
        for step_x in range(3):
            for step_y in range(3):
                summed = (
                    summed
                    + conv_weight[9 * step_z + 3 * step_x + step_y]
                    * padded[
                        step_z : step_z + z_count,
                        step_x : step_x + x_count,
                        step_y : step_y + slab_y,
                    ]
                )
    positioned = summed.astype(jnp.bfloat16)
    local_tok = z_count * x_count * y_count
    heads_here = qkv_weight.shape[0] // (3 * HS)
    slab_rows = (
        positioned.reshape(z_count, x_count, groups, y_count, features)
        .transpose(2, 0, 1, 3, 4)
        .reshape(groups * local_tok, features)
    )
    slab_tok = slab_rows.shape[0]
    projected = times_transposed(slab_rows, qkv_weight).astype(jnp.bfloat16)
    split_heads = projected.reshape(slab_tok, heads_here, 3, HS)
    queries = split_heads[:, :, 0]
    key_value = relayed(split_heads[:, :, 1:], "blk")
    key_piece = key_value[:, :, 0]
    value_piece = key_value[:, :, 1]
    score_scale = 1.0 / math.sqrt(HS)
    key_count = key_piece.shape[0]
    block_len = min(1024, key_count)
    key_blocks = key_piece.reshape(key_count // block_len, block_len, heads_here, HS)
    value_blocks = value_piece.reshape(key_count // block_len, block_len, heads_here, HS)

    def attend(query_rows):
        rows = query_rows.shape[0]

        def key_block(carry_state, key_value):
            running_max, running_sum, weighted = carry_state
            key_part, value_part = key_value
            scores = (
                jnp.einsum(
                    "qhd,khd->hqk", query_rows, key_part, preferred_element_type=jnp.float32
                )
                * score_scale
            )
            new_max = jnp.maximum(running_max, jnp.max(scores, axis=2))
            shrink = jnp.exp(running_max - new_max)
            weights = jnp.exp(scores - new_max[:, :, None])
            running_sum = running_sum * shrink + jnp.sum(weights, axis=2)
            weighted = weighted * shrink[:, :, None] + jnp.einsum(
                "hqk,khd->hqd",
                weights.astype(jnp.bfloat16),
                value_part,
                preferred_element_type=jnp.float32,
            )
            return ((new_max, running_sum, weighted), None)

        start_state = (
            jnp.full((heads_here, rows), -1e30, jnp.float32),
            jnp.zeros((heads_here, rows), jnp.float32),
            jnp.zeros((heads_here, rows, HS), jnp.float32),
        )
        folded, unused = lax.scan(key_block, start_state, (key_blocks, value_blocks))
        running_max, running_sum, weighted = folded
        attended = (weighted / running_sum[:, :, None]).astype(jnp.bfloat16)
        return attended.transpose(1, 0, 2).reshape(rows, heads_here * HS)

    rank = lax.axis_index("uly")
    chips, core, chip = groups // 2, rank % 2, rank // 2
    pair_queries = queries.reshape(chips, 2 * local_tok, heads_here, HS)
    total = None
    for shift in range(1, chips):
        far_rows = lax.dynamic_index_in_dim(pair_queries, (chip + shift) % chips, 0, keepdims=False)
        far_partial = jnp.dot(attend(far_rows), out_weight, preferred_element_type=jnp.float32)
        far_partial = far_partial.astype(jnp.bfloat16).reshape(2, local_tok, features)
        same_core = lax.dynamic_index_in_dim(far_partial, core, 0, keepdims=False)
        other_core = lax.dynamic_index_in_dim(far_partial, 1 - core, 0, keepdims=False)
        out_layout = Layout(major_to_minor=tuple(range(tokens.ndim)))
        same_core = with_layout_constraint(same_core.reshape(tokens.shape), out_layout)
        other_core = with_layout_constraint(other_core.reshape(tokens.shape), out_layout)
        far_sent = (same_core, other_core)
        to_other_core = [
            (i, ((i // 2 + shift) % chips) * 2 + 1 - i % 2) for i in range(groups)
        ]
        for arrived in (
            lax.ppermute(same_core, "uly", chip_shift(groups, shift)),
            lax.ppermute(other_core, "uly", to_other_core),
        ):
            arrived = arrived.astype(jnp.float32).reshape(tokens.shape)
            total = arrived if total is None else total + arrived
    near_rows = lax.dynamic_index_in_dim(pair_queries, chip, 0, keepdims=False)
    if total is not None:
        near_rows, unused = lax.optimization_barrier((near_rows, far_sent))
    near_partial = jnp.dot(attend(near_rows), out_weight, preferred_element_type=jnp.float32)
    near_partial = near_partial.reshape(2, local_tok, features)
    own = lax.dynamic_index_in_dim(near_partial, core, 0, keepdims=False)
    for_partner = lax.dynamic_index_in_dim(near_partial, 1 - core, 0, keepdims=False)
    from_partner = lax.ppermute(for_partner, "uly", [(i, i ^ 1) for i in range(groups)])
    near_sum = own.reshape(tokens.shape) + from_partner.reshape(tokens.shape)
    near_sum = with_layout_constraint(near_sum, Layout(major_to_minor=tuple(range(tokens.ndim))))
    result = near_sum if total is None else near_sum + total
    return result.astype(jnp.bfloat16)


def solution(mesh):
    in_specs = (P("blk", None, "uly", None), P(), P(), P("uly", None), P("uly", None))
    out_specs = P("blk", None, "uly", None)
    return jax.shard_map(
        on_device, mesh=mesh, in_specs=in_specs, out_specs=out_specs, check_vma=False
    )
```

```python
import math

import jax
import jax.numpy as jnp
from jax import lax
from jax.experimental.layout import Layout, with_layout_constraint
from jax.sharding import PartitionSpec as P

HS = 64


def padded_2(shard, sides, width, keep=None):
    for axis, dim in sides:
        size, length = (lax.axis_size(axis), shard.shape[dim])
        up = [(i, (i + 1) % size) for i in range(size - 1)]
        down = [(j, i) for i, j in up]
        last = lax.slice_in_dim(shard, length - width, length, axis=dim)
        initial = lax.slice_in_dim(shard, 0, width, axis=dim)
        if keep is not None:
            last = with_layout_constraint(last, keep)
            initial = with_layout_constraint(initial, keep)
        before = lax.ppermute(last, axis, up)
        after = lax.ppermute(initial, axis, down)
        shard = jnp.concatenate([before, shard, after], axis=dim)
    return shard


def gathered(piece, axis):
    size = lax.axis_size(axis)
    parts = [piece]
    for shift in range(1, size):
        pairs = [(i, (i + shift) % size) for i in range(size)]
        parts.append(lax.ppermute(piece, axis, pairs))
    return jnp.concatenate(parts, axis=0)


def relayed(piece, axis):
    size = lax.axis_size(axis)
    half = size // 2
    if size % 2:
        return gathered(piece, axis)
    mirror = [(i, (i + half) % size) for i in range(size)]
    crossed = lax.ppermute(piece, axis, mirror)
    parts = [piece, crossed]
    for shift in range(1, half):
        pairs = [(i, (i // half) * half + (i % half + shift) % half) for i in range(size)]
        parts.append(lax.ppermute(piece, axis, pairs))
        parts.append(lax.ppermute(crossed, axis, pairs))
    return jnp.concatenate(parts, axis=0)


def chip_shift(size, shift):
    chips = size // 2
    return [(i, ((i // 2 + shift) % chips) * 2 + i % 2) for i in range(size)]


def gathered_by_chip(piece, axis):
    size = lax.axis_size(axis)
    rank = lax.axis_index(axis)
    chips, core = size // 2, rank % 2
    partner = [(i, i ^ 1) for i in range(size)]
    stacked = jnp.zeros((size,) + piece.shape, piece.dtype)
    stacked = lax.dynamic_update_index_in_dim(stacked, piece, rank, 0)
    near = lax.ppermute(piece, axis, partner)
    stacked = lax.dynamic_update_index_in_dim(stacked, near, rank ^ 1, 0)
    for shift in range(1, chips):
        source_chip = (rank // 2 - shift) % chips
        far = lax.ppermute(piece, axis, chip_shift(size, shift))
        stacked = lax.dynamic_update_index_in_dim(stacked, far, source_chip * 2 + core, 0)
        handed = lax.ppermute(far, axis, partner)
        stacked = lax.dynamic_update_index_in_dim(stacked, handed, source_chip * 2 + 1 - core, 0)
    return stacked


def scattered_sum_by_chip(whole, axis, shape):
    size = lax.axis_size(axis)
    rank = lax.axis_index(axis)
    chips, core, chip = size // 2, rank % 2, rank // 2
    blocks = whole.reshape(chips, 2, whole.shape[0] // size, *whole.shape[1:])
    mine = lax.dynamic_index_in_dim(blocks, core, 1, keepdims=False)
    theirs = lax.dynamic_index_in_dim(blocks, 1 - core, 1, keepdims=False)
    chip_sum = mine + lax.ppermute(theirs, axis, [(i, i ^ 1) for i in range(size)])
    total = lax.dynamic_index_in_dim(chip_sum, chip, 0, keepdims=False).reshape(shape)
    for shift in range(1, chips):
        outgoing = lax.dynamic_index_in_dim(chip_sum, (chip + shift) % chips, 0, keepdims=False)
        arrived = lax.ppermute(outgoing.astype(jnp.bfloat16), axis, chip_shift(size, shift))
        total = total + arrived.astype(jnp.float32).reshape(shape)
    return total


def scattered_sum(whole, axis):
    size = lax.axis_size(axis)
    rank = lax.axis_index(axis)
    blocks = whole.reshape(size, whole.shape[0] // size, *whole.shape[1:])
    total = lax.dynamic_index_in_dim(blocks, rank, 0, keepdims=False)
    for shift in range(1, size):
        pairs = [(i, (i + shift) % size) for i in range(size)]
        outgoing = lax.dynamic_index_in_dim(blocks, (rank + shift) % size, 0, keepdims=False)
        total = total + lax.ppermute(outgoing, axis, pairs)
    return total


def times_transposed(left, right):
    return lax.dot_general(
        left, right, (((1,), (1,)), ((), ())), preferred_element_type=jnp.float32
    )


def on_device(tokens, conv_weight, conv_bias, qkv_weight, out_weight):
    z_count, x_count, y_count, features = tokens.shape
    groups = lax.axis_size("uly")
    arrival = Layout(major_to_minor=tuple(range(tokens.ndim)))
    with_halo = padded_2(tokens, (("blk", 0),), 1, arrival if y_count == 2 else None)
    slab_in = gathered_by_chip(with_halo, "uly")
    slab_in = slab_in.transpose(1, 2, 0, 3, 4).reshape(
        z_count + 2, x_count, groups * y_count, features
    )
    slab_y = groups * y_count
    padded = jnp.pad(slab_in, ((0, 0), (1, 1), (1, 1), (0, 0)))
    summed = slab_in[1 : 1 + z_count].astype(jnp.float32) + conv_bias
    for step_z in range(3):
        for step_x in range(3):
            for step_y in range(3):
                summed = (
                    summed
                    + conv_weight[9 * step_z + 3 * step_x + step_y]
                    * padded[
                        step_z : step_z + z_count,
                        step_x : step_x + x_count,
                        step_y : step_y + slab_y,
                    ]
                )
    positioned = summed.astype(jnp.bfloat16)
    local_tok = z_count * x_count * y_count
    heads_here = qkv_weight.shape[0] // (3 * HS)
    slab_rows = (
        positioned.reshape(z_count, x_count, groups, y_count, features)
        .transpose(2, 0, 1, 3, 4)
        .reshape(groups * local_tok, features)
    )
    slab_tok = slab_rows.shape[0]
    projected = times_transposed(slab_rows, qkv_weight).astype(jnp.bfloat16)
    split_heads = projected.reshape(slab_tok, heads_here, 3, HS)
    queries = split_heads[:, :, 0]
    key_value = relayed(split_heads[:, :, 1:], "blk")
    key_piece = key_value[:, :, 0]
    value_piece = key_value[:, :, 1]
    score_scale = 1.0 / math.sqrt(HS)
    key_count = key_piece.shape[0]
    block_len = min(1024, key_count)
    key_blocks = key_piece.reshape(key_count // block_len, block_len, heads_here, HS)
    value_blocks = value_piece.reshape(key_count // block_len, block_len, heads_here, HS)

    def attend(query_rows):
        rows = query_rows.shape[0]

        def key_block(carry_state, key_value):
            running_max, running_sum, weighted = carry_state
            key_part, value_part = key_value
            scores = (
                jnp.einsum(
                    "qhd,khd->hqk", query_rows, key_part, preferred_element_type=jnp.float32
                )
                * score_scale
            )
            new_max = jnp.maximum(running_max, jnp.max(scores, axis=2))
            shrink = jnp.exp(running_max - new_max)
            weights = jnp.exp(scores - new_max[:, :, None])
            running_sum = running_sum * shrink + jnp.sum(weights, axis=2)
            weighted = weighted * shrink[:, :, None] + jnp.einsum(
                "hqk,khd->hqd",
                weights.astype(jnp.bfloat16),
                value_part,
                preferred_element_type=jnp.float32,
            )
            return ((new_max, running_sum, weighted), None)

        if key_blocks.shape[0] == 1:
            scores = (
                jnp.einsum(
                    "qhd,khd->hqk", query_rows, key_piece, preferred_element_type=jnp.float32
                )
                * score_scale
            )
            row_max = jnp.max(scores, axis=2, keepdims=True)
            weights = jnp.exp(scores - row_max)
            row_sum = jnp.sum(weights, axis=2, keepdims=True)
            mixed = jnp.einsum(
                "hqk,khd->hqd",
                weights.astype(jnp.bfloat16),
                value_piece,
                preferred_element_type=jnp.float32,
            )
            attended = (mixed / row_sum).astype(jnp.bfloat16)
            return attended.transpose(1, 0, 2).reshape(rows, heads_here * HS)

        start_state = (
            jnp.full((heads_here, rows), -1e30, jnp.float32),
            jnp.zeros((heads_here, rows), jnp.float32),
            jnp.zeros((heads_here, rows, HS), jnp.float32),
        )
        folded, unused = lax.scan(key_block, start_state, (key_blocks, value_blocks))
        running_max, running_sum, weighted = folded
        attended = (weighted / running_sum[:, :, None]).astype(jnp.bfloat16)
        return attended.transpose(1, 0, 2).reshape(rows, heads_here * HS)

    rank = lax.axis_index("uly")
    chips, core, chip = groups // 2, rank % 2, rank // 2
    pair_queries = queries.reshape(chips, 2 * local_tok, heads_here, HS)
    total = None
    for shift in range(1, chips):
        far_rows = lax.dynamic_index_in_dim(pair_queries, (chip + shift) % chips, 0, keepdims=False)
        far_partial = jnp.dot(attend(far_rows), out_weight, preferred_element_type=jnp.float32)
        far_partial = far_partial.astype(jnp.bfloat16).reshape(2, local_tok, features)
        same_core = lax.dynamic_index_in_dim(far_partial, core, 0, keepdims=False)
        other_core = lax.dynamic_index_in_dim(far_partial, 1 - core, 0, keepdims=False)
        far_sent = (same_core, other_core)
        to_other_core = [
            (i, ((i // 2 + shift) % chips) * 2 + 1 - i % 2) for i in range(groups)
        ]
        for arrived in (
            lax.ppermute(same_core, "uly", chip_shift(groups, shift)),
            lax.ppermute(other_core, "uly", to_other_core),
        ):
            arrived = arrived.astype(jnp.float32).reshape(tokens.shape)
            total = arrived if total is None else total + arrived
    near_rows = lax.dynamic_index_in_dim(pair_queries, chip, 0, keepdims=False)
    if total is not None:
        near_rows, unused = lax.optimization_barrier((near_rows, far_sent))
    near_partial = jnp.dot(attend(near_rows), out_weight, preferred_element_type=jnp.float32)
    near_partial = near_partial.reshape(2, local_tok, features)
    own = lax.dynamic_index_in_dim(near_partial, core, 0, keepdims=False)
    for_partner = lax.dynamic_index_in_dim(near_partial, 1 - core, 0, keepdims=False)
    from_partner = lax.ppermute(for_partner, "uly", [(i, i ^ 1) for i in range(groups)])
    near_sum = own.reshape(tokens.shape) + from_partner.reshape(tokens.shape)
    result = near_sum if total is None else near_sum + total
    return result.astype(jnp.bfloat16)


def solution(mesh):
    in_specs = (P("blk", None, "uly", None), P(), P(), P("uly", None), P("uly", None))
    out_specs = P("blk", None, "uly", None)
    return jax.shard_map(
        on_device, mesh=mesh, in_specs=in_specs, out_specs=out_specs, check_vma=False
    )
```

```python
import math

import jax
import jax.numpy as jnp
from jax import lax
from jax.experimental.layout import Layout, with_layout_constraint
from jax.sharding import PartitionSpec as P

HS = 64


def padded_2(shard, sides, width, keep=None):
    for axis, dim in sides:
        size, length = (lax.axis_size(axis), shard.shape[dim])
        up = [(i, (i + 1) % size) for i in range(size - 1)]
        down = [(j, i) for i, j in up]
        last = lax.slice_in_dim(shard, length - width, length, axis=dim)
        initial = lax.slice_in_dim(shard, 0, width, axis=dim)
        if keep is not None:
            last = with_layout_constraint(last, keep)
            initial = with_layout_constraint(initial, keep)
        before = lax.ppermute(last, axis, up)
        after = lax.ppermute(initial, axis, down)
        shard = jnp.concatenate([before, shard, after], axis=dim)
    return shard


def gathered(piece, axis):
    size = lax.axis_size(axis)
    parts = [piece]
    for shift in range(1, size):
        pairs = [(i, (i + shift) % size) for i in range(size)]
        parts.append(lax.ppermute(piece, axis, pairs))
    return jnp.concatenate(parts, axis=0)


def relayed(piece, axis):
    size = lax.axis_size(axis)
    half = size // 2
    if size % 2:
        return gathered(piece, axis)
    mirror = [(i, (i + half) % size) for i in range(size)]
    crossed = lax.ppermute(piece, axis, mirror)
    parts = [piece, crossed]
    for shift in range(1, half):
        pairs = [(i, (i // half) * half + (i % half + shift) % half) for i in range(size)]
        parts.append(lax.ppermute(piece, axis, pairs))
        parts.append(lax.ppermute(crossed, axis, pairs))
    return jnp.concatenate(parts, axis=0)


def chip_shift(size, shift):
    chips = size // 2
    return [(i, ((i // 2 + shift) % chips) * 2 + i % 2) for i in range(size)]


def gathered_by_chip(piece, axis):
    size = lax.axis_size(axis)
    rank = lax.axis_index(axis)
    chips, core = size // 2, rank % 2
    partner = [(i, i ^ 1) for i in range(size)]
    stacked = jnp.zeros((size,) + piece.shape, piece.dtype)
    stacked = lax.dynamic_update_index_in_dim(stacked, piece, rank, 0)
    near = lax.ppermute(piece, axis, partner)
    stacked = lax.dynamic_update_index_in_dim(stacked, near, rank ^ 1, 0)
    for shift in range(1, chips):
        source_chip = (rank // 2 - shift) % chips
        far = lax.ppermute(piece, axis, chip_shift(size, shift))
        stacked = lax.dynamic_update_index_in_dim(stacked, far, source_chip * 2 + core, 0)
        handed = lax.ppermute(far, axis, partner)
        stacked = lax.dynamic_update_index_in_dim(stacked, handed, source_chip * 2 + 1 - core, 0)
    return stacked


def scattered_sum_by_chip(whole, axis, shape):
    size = lax.axis_size(axis)
    rank = lax.axis_index(axis)
    chips, core, chip = size // 2, rank % 2, rank // 2
    blocks = whole.reshape(chips, 2, whole.shape[0] // size, *whole.shape[1:])
    mine = lax.dynamic_index_in_dim(blocks, core, 1, keepdims=False)
    theirs = lax.dynamic_index_in_dim(blocks, 1 - core, 1, keepdims=False)
    chip_sum = mine + lax.ppermute(theirs, axis, [(i, i ^ 1) for i in range(size)])
    total = lax.dynamic_index_in_dim(chip_sum, chip, 0, keepdims=False).reshape(shape)
    for shift in range(1, chips):
        outgoing = lax.dynamic_index_in_dim(chip_sum, (chip + shift) % chips, 0, keepdims=False)
        arrived = lax.ppermute(outgoing.astype(jnp.bfloat16), axis, chip_shift(size, shift))
        total = total + arrived.astype(jnp.float32).reshape(shape)
    return total


def scattered_sum(whole, axis):
    size = lax.axis_size(axis)
    rank = lax.axis_index(axis)
    blocks = whole.reshape(size, whole.shape[0] // size, *whole.shape[1:])
    total = lax.dynamic_index_in_dim(blocks, rank, 0, keepdims=False)
    for shift in range(1, size):
        pairs = [(i, (i + shift) % size) for i in range(size)]
        outgoing = lax.dynamic_index_in_dim(blocks, (rank + shift) % size, 0, keepdims=False)
        total = total + lax.ppermute(outgoing, axis, pairs)
    return total


def times_transposed(left, right):
    return lax.dot_general(
        left, right, (((1,), (1,)), ((), ())), preferred_element_type=jnp.float32
    )


def on_device(tokens, conv_weight, conv_bias, qkv_weight, out_weight):
    z_count, x_count, y_count, features = tokens.shape
    groups = lax.axis_size("uly")
    arrival = Layout(major_to_minor=tuple(range(tokens.ndim)))
    with_halo = padded_2(tokens, (("blk", 0),), 1, arrival if y_count == 2 else None)
    slab_in = gathered_by_chip(with_halo, "uly")
    slab_in = slab_in.transpose(1, 2, 0, 3, 4).reshape(
        z_count + 2, x_count, groups * y_count, features
    )
    slab_y = groups * y_count
    padded = jnp.pad(slab_in, ((0, 0), (1, 1), (1, 1), (0, 0)))
    summed = slab_in[1 : 1 + z_count].astype(jnp.float32) + conv_bias
    for step_z in range(3):
        for step_x in range(3):
            for step_y in range(3):
                summed = (
                    summed
                    + conv_weight[9 * step_z + 3 * step_x + step_y]
                    * padded[
                        step_z : step_z + z_count,
                        step_x : step_x + x_count,
                        step_y : step_y + slab_y,
                    ]
                )
    positioned = summed.astype(jnp.bfloat16)
    local_tok = z_count * x_count * y_count
    heads_here = qkv_weight.shape[0] // (3 * HS)
    slab_rows = (
        positioned.reshape(z_count, x_count, groups, y_count, features)
        .transpose(2, 0, 1, 3, 4)
        .reshape(groups * local_tok, features)
    )
    slab_tok = slab_rows.shape[0]
    projected = times_transposed(slab_rows, qkv_weight).astype(jnp.bfloat16)
    projected = with_layout_constraint(projected, Layout(major_to_minor=(1, 0)))
    split_heads = projected.reshape(slab_tok, heads_here, 3, HS)
    queries = split_heads[:, :, 0]
    key_value = relayed(split_heads[:, :, 1:], "blk")
    key_piece = key_value[:, :, 0]
    value_piece = key_value[:, :, 1]
    score_scale = 1.0 / math.sqrt(HS)
    key_count = key_piece.shape[0]
    block_len = min(1024, key_count)
    key_blocks = key_piece.reshape(key_count // block_len, block_len, heads_here, HS)
    value_blocks = value_piece.reshape(key_count // block_len, block_len, heads_here, HS)

    def attend(query_rows):
        rows = query_rows.shape[0]

        def key_block(carry_state, key_value):
            running_max, running_sum, weighted = carry_state
            key_part, value_part = key_value
            scores = (
                jnp.einsum(
                    "qhd,khd->hqk", query_rows, key_part, preferred_element_type=jnp.float32
                )
                * score_scale
            )
            new_max = jnp.maximum(running_max, jnp.max(scores, axis=2))
            shrink = jnp.exp(running_max - new_max)
            weights = jnp.exp(scores - new_max[:, :, None])
            running_sum = running_sum * shrink + jnp.sum(weights, axis=2)
            weighted = weighted * shrink[:, :, None] + jnp.einsum(
                "hqk,khd->hqd",
                weights.astype(jnp.bfloat16),
                value_part,
                preferred_element_type=jnp.float32,
            )
            return ((new_max, running_sum, weighted), None)

        if key_blocks.shape[0] == 1:
            scores = (
                jnp.einsum(
                    "qhd,khd->hqk", query_rows, key_piece, preferred_element_type=jnp.float32
                )
                * score_scale
            )
            row_max = jnp.max(scores, axis=2, keepdims=True)
            weights = jnp.exp(scores - row_max)
            row_sum = jnp.sum(weights, axis=2, keepdims=True)
            mixed = jnp.einsum(
                "hqk,khd->hqd",
                weights.astype(jnp.bfloat16),
                value_piece,
                preferred_element_type=jnp.float32,
            )
            attended = (mixed / row_sum).astype(jnp.bfloat16)
            return attended.transpose(1, 0, 2).reshape(rows, heads_here * HS)

        start_state = (
            jnp.full((heads_here, rows), -1e30, jnp.float32),
            jnp.zeros((heads_here, rows), jnp.float32),
            jnp.zeros((heads_here, rows, HS), jnp.float32),
        )
        folded, unused = lax.scan(key_block, start_state, (key_blocks, value_blocks))
        running_max, running_sum, weighted = folded
        attended = (weighted / running_sum[:, :, None]).astype(jnp.bfloat16)
        return attended.transpose(1, 0, 2).reshape(rows, heads_here * HS)

    rank = lax.axis_index("uly")
    chips, core, chip = groups // 2, rank % 2, rank // 2
    pair_queries = queries.reshape(chips, 2 * local_tok, heads_here, HS)
    total = None
    for shift in range(1, chips):
        far_rows = lax.dynamic_index_in_dim(pair_queries, (chip + shift) % chips, 0, keepdims=False)
        far_partial = jnp.dot(attend(far_rows), out_weight, preferred_element_type=jnp.float32)
        far_partial = far_partial.astype(jnp.bfloat16).reshape(2, local_tok, features)
        same_core = lax.dynamic_index_in_dim(far_partial, core, 0, keepdims=False)
        other_core = lax.dynamic_index_in_dim(far_partial, 1 - core, 0, keepdims=False)
        far_sent = (same_core, other_core)
        to_other_core = [
            (i, ((i // 2 + shift) % chips) * 2 + 1 - i % 2) for i in range(groups)
        ]
        for arrived in (
            lax.ppermute(same_core, "uly", chip_shift(groups, shift)),
            lax.ppermute(other_core, "uly", to_other_core),
        ):
            arrived = arrived.astype(jnp.float32).reshape(tokens.shape)
            total = arrived if total is None else total + arrived
    near_rows = lax.dynamic_index_in_dim(pair_queries, chip, 0, keepdims=False)
    if total is not None:
        near_rows, unused = lax.optimization_barrier((near_rows, far_sent))
    near_partial = jnp.dot(attend(near_rows), out_weight, preferred_element_type=jnp.float32)
    near_partial = near_partial.reshape(2, local_tok, features)
    own = lax.dynamic_index_in_dim(near_partial, core, 0, keepdims=False)
    for_partner = lax.dynamic_index_in_dim(near_partial, 1 - core, 0, keepdims=False)
    from_partner = lax.ppermute(for_partner, "uly", [(i, i ^ 1) for i in range(groups)])
    near_sum = own.reshape(tokens.shape) + from_partner.reshape(tokens.shape)
    result = near_sum if total is None else near_sum + total
    return result.astype(jnp.bfloat16)


def solution(mesh):
    in_specs = (P("blk", None, "uly", None), P(), P(), P("uly", None), P("uly", None))
    out_specs = P("blk", None, "uly", None)
    return jax.shard_map(
        on_device, mesh=mesh, in_specs=in_specs, out_specs=out_specs, check_vma=False
    )
```
